32 devices in a mesh: band: 4 (over z), gy: 2 (over x), gz: 4 (over y, core).
Axes of the slice: x: 2, y: 2, z: 4, core: 2. Of those that a mesh axis runs over, the one named last changes fastest.
Arguments:
- i_coeff: float32 [4, 96, 96, 96], P('band', 'gy', 'gz'), may hold values from -6 to 6
- j_coeff: float32 [8, 96, 96, 96], P('band', 'gy', 'gz'), may hold values from -6 to 6
- pair_orbital: int32 [4, 1], P('band'), may hold values from 0 to 7
- pair_occ: int32 [4, 1], P('band'), may hold values from 1 to 2
Outputs:
- exchange_applied: float32 [4, 96, 96, 96], P('band', 'gy', 'gz')
- pair_energy: float32 [4, 1], P('band')
The draws below stay inside these ranges and needn't reach their ends.
All inputs are finite; a program needn't handle non-finite values.
Results may differ from the reference program's by a relative error of at most 0.00022.
Values sent between devices are 32-bit elements; how exact they have to be, the bound alone decides.
No kernel may reach another device: no remote copies, remote signals or barrier semaphores. Data moves between devices by JAX's collectives and lax.ppermute only.
A program may use at most 64 MiB of HBM per device.

```python
import math
import jax
import jax.numpy as jnp
import numpy as np
from jax import lax

N = 96
NJ = 8
BAND_I = 4
PK = 1


def with_ends(entries, rng, least, largest):
    longest = entries.shape.index(max(entries.shape))
    spots = []
    for shift in (0, 1):
        where = [jax.random.randint(jax.random.fold_in(rng, axis), (), 0, length) for axis, length in enumerate(entries.shape)]
        where[longest] = (where[longest] + shift) % entries.shape[longest]
        spots.append(tuple(where))
    return entries.at[spots[0]].set(least).at[spots[1]].set(largest)


def steps_of(key, shape, shards, low, high):
    def one(dim, parts):
        steps = jax.random.uniform(jax.random.fold_in(jax.random.fold_in(key, 6), dim), (parts,), jnp.float32, low / len(shards), high / len(shards))
        return jnp.repeat(jnp.exp(steps), shape[dim] // parts).reshape((-1,) + (1,) * (len(shape) - dim - 1))

    loudness = one(*shards[0])
    for cut in shards[1:]:
        loudness = loudness * one(*cut)
    return loudness


def centred(key, shape, deviation, bound, pieces=(), kind=jnp.bfloat16):
    loudness = steps_of(key, shape, pieces, -0.22, 0.18) if pieces else 1.0
    drawn = jax.random.normal(key, shape, jnp.float32) * deviation * loudness
    return jnp.minimum(jnp.maximum(drawn, -bound), bound).astype(kind)


def setup_inputs(seed: int = 0) -> dict:
    keys = jax.random.split(jax.random.key(seed), 5)
    i_coeff = centred(keys[0], (BAND_I, N, N, N), 1.0, 6.0, ((0, 4), (1, 2), (2, 4)), jnp.float32)
    j_coeff = centred(keys[1], (NJ, N, N, N), 1.0, 6.0, ((0, 4), (1, 2), (2, 4)), jnp.float32)
    pair_orbital = with_ends(jax.random.randint(keys[2], (BAND_I, PK), 0, NJ), jax.random.fold_in(keys[2], 1), 0, NJ - 1).astype(jnp.int32)
    pair_occ = with_ends(jax.random.randint(keys[3], (BAND_I, PK), 1, 3), jax.random.fold_in(keys[3], 1), 1, 2).astype(jnp.int32)
    return dict(i_coeff=i_coeff, j_coeff=j_coeff, pair_orbital=pair_orbital, pair_occ=pair_occ)


tap_offsets = np.arange(-8, 8)
raw_taps = 0.6 ** np.abs(tap_offsets + 0.5) * np.where(tap_offsets % 2 == 0, 1.0, -0.6)
FILTER_TAPS = raw_taps / np.sqrt(np.sum(raw_taps ** 2))
SCREEN = 0.001

def filter_along(field, axis_number):
    widths = [(0, 0)] * field.ndim
    widths[axis_number] = (8, 8)
    padded = jnp.pad(field, widths)
    extent = field.shape[axis_number]
    result = jnp.zeros(field.shape, jnp.float32)
    for number in range(16):
        result = result + float(FILTER_TAPS[number]) * lax.slice_in_dim(padded, number, number + extent, axis=axis_number)
    return result

def synthesize(coeff):
    return filter_along(filter_along(filter_along(coeff, 1), 2), 3)

def potential_of(density):
    period = 2 * N
    padded = jnp.pad(density, ((0, N), (0, N), (0, N)))
    frequency = jnp.arange(period).astype(jnp.float32)
    lattice = 2.0 - 2.0 * jnp.cos(2.0 * math.pi / period * frequency)
    kernel = 1.0 / (lattice[:, None, None] + lattice[None, :, None] + lattice[None, None, :] + SCREEN)
    spectrum = jnp.fft.fftn(padded) * kernel
    return jnp.real(jnp.fft.ifftn(spectrum))[:N, :N, :N].astype(jnp.float32)

def reference(i_coeff, j_coeff, pair_orbital, pair_occ):
    first_set = synthesize(i_coeff)
    second = synthesize(j_coeff)
    applied_rows = []
    energy_rows = []
    for row_number in range(first_set.shape[0]):
        own_field = first_set[row_number]
        applied = jnp.zeros(own_field.shape, jnp.float32)
        energies = []
        for column in range(pair_orbital.shape[1]):
            partner = second[pair_orbital[row_number, column]]
            density = own_field * partner
            potential = potential_of(density)
            energies.append(jnp.mean(density * potential))
            applied = applied - pair_occ[row_number, column].astype(jnp.float32) * potential * partner
        applied_rows.append(applied)
        energy_rows.append(jnp.stack(energies))
    return (jnp.stack(applied_rows), jnp.stack(energy_rows))
```

```python
import math

import jax
import jax.numpy as jnp
import numpy as np
from jax import lax
from jax.sharding import PartitionSpec as P

tap_offsets = np.arange(-8, 8)
raw_taps = 0.6 ** np.abs(tap_offsets + 0.5) * np.where(tap_offsets % 2 == 0, 1.0, -0.6)
FILTER_TAPS = raw_taps / np.sqrt(np.sum(raw_taps**2))
SCREEN = 0.001
precise_mode = lax.Precision.HIGHEST


def extended(cells, sides, width):
    for axis, dim in sides:
        count = lax.axis_size(axis)
        ends = count - 1
        head = lax.slice_in_dim(cells, 0, width, axis=dim)
        tail = lax.slice_in_dim(cells, cells.shape[dim] - width, cells.shape[dim], axis=dim)
        cells = jnp.concatenate(
            [
                lax.ppermute(tail, axis, [(i, (i + 1) % count) for i in range(ends)]),
                cells,
                lax.ppermute(head, axis, [((i + 1) % count, i) for i in range(ends)]),
            ],
            axis=dim,
        )
    return cells


def band_matrix(row_count, col_count, shift_by):
    row_index = jnp.arange(row_count, dtype=jnp.int32)[:, None]
    col_index = jnp.arange(col_count, dtype=jnp.int32)[None, :]
    offset = row_index - shift_by - col_index
    picked = jnp.zeros((row_count, col_count), jnp.float32)
    for number in range(16):
        picked = picked + jnp.where(offset == number - 8, float(FILTER_TAPS[number]), 0.0)
    return picked


def synthesize(padded):
    wide_y, wide_z, length = (padded.shape[1], padded.shape[2], padded.shape[3])
    matrix_y = band_matrix(wide_y, wide_y - 16, 8)
    matrix_z = band_matrix(wide_z, wide_z - 16, 8)
    matrix_x = band_matrix(length, length, 0)
    step_one = jnp.einsum("oqzx,qy->oyzx", padded, matrix_y, precision=precise_mode)
    step_two = jnp.einsum("oyqx,qz->oyzx", step_one, matrix_z, precision=precise_mode)
    return jnp.matmul(step_two, matrix_x, precision=precise_mode)


def dft_tables(length, period):
    positions = (
        jnp.arange(length, dtype=jnp.int32)[:, None] * jnp.arange(period, dtype=jnp.int32)[None, :]
    )
    angles = 2.0 * math.pi / period * (positions % period).astype(jnp.float32)
    return (jnp.cos(angles), jnp.sin(angles))


def spectral_weights(first_index, second_index, third_index, period):

    def lattice(positions):
        angles = 2.0 * math.pi / period * (positions % period).astype(jnp.float32)
        return 2.0 - 2.0 * jnp.cos(angles)

    return 1.0 / (
        lattice(first_index)[:, None, None]
        + lattice(second_index)[None, :, None]
        + lattice(third_index)[None, None, :]
        + SCREEN
    )


def transform(real_part, imag_part, cosine_table, sine_table, einsum_form, direction):
    new_real = jnp.einsum(
        einsum_form, real_part, cosine_table, precision=precise_mode
    ) + direction * jnp.einsum(einsum_form, imag_part, sine_table, precision=precise_mode)
    new_imag = jnp.einsum(
        einsum_form, imag_part, cosine_table, precision=precise_mode
    ) - direction * jnp.einsum(einsum_form, real_part, sine_table, precision=precise_mode)
    return (new_real, new_imag)


def first_section(density_real, density_imag, cosine_table, sine_table):
    real_part = jnp.matmul(density_real, cosine_table, precision=precise_mode) + jnp.matmul(
        density_imag, sine_table, precision=precise_mode
    )
    imag_part = jnp.matmul(density_imag, cosine_table, precision=precise_mode) - jnp.matmul(
        density_real, sine_table, precision=precise_mode
    )
    return (real_part, imag_part)


def last_section(real_part, imag_part, cosine_table, sine_table, period):
    scale_by = 1.0 / float(period**3)
    result_real = (
        jnp.matmul(real_part, cosine_table.T, precision=precise_mode)
        - jnp.matmul(imag_part, sine_table.T, precision=precise_mode)
    ) * scale_by
    result_imag = (
        jnp.matmul(imag_part, cosine_table.T, precision=precise_mode)
        + jnp.matmul(real_part, sine_table.T, precision=precise_mode)
    ) * scale_by
    return (result_real, result_imag)


def slab_potential(density_real, density_imag):
    pair_count, rows_y, rows_z, length = density_real.shape
    period = 2 * length
    cosine_table, sine_table = dft_tables(length, period)
    count_y = lax.axis_size("gy")
    count_z = lax.axis_size("gz")
    spread = count_y * count_z
    width_x = period // spread
    real_part, imag_part = first_section(density_real, density_imag, cosine_table, sine_table)
    packed = jnp.stack((real_part, imag_part), 1).reshape(pair_count, 2, rows_y * rows_z, period)
    arrived = lax.all_to_all(packed, ("gy", "gz"), split_axis=3, concat_axis=2, tiled=True)
    arrived = arrived.reshape(pair_count, 2, count_y, count_z, rows_y, rows_z, width_x)
    arrived = arrived.transpose(0, 1, 6, 2, 4, 3, 5).reshape(
        pair_count, 2, width_x, count_y * rows_y, count_z * rows_z
    )
    real_part, imag_part = transform(
        arrived[:, 0], arrived[:, 1], cosine_table, sine_table, "pkyz,yq->pkqz", 1.0
    )
    real_part, imag_part = transform(
        real_part, imag_part, cosine_table, sine_table, "pkqz,zr->pkqr", 1.0
    )
    first_index = lax.axis_index(("gy", "gz")) * width_x + jnp.arange(width_x, dtype=jnp.int32)
    all_freq = jnp.arange(period, dtype=jnp.int32)
    kernel = spectral_weights(first_index, all_freq, all_freq, period)
    real_part = real_part * kernel
    imag_part = imag_part * kernel
    real_part, imag_part = transform(
        real_part, imag_part, cosine_table.T, sine_table.T, "pkqr,rz->pkqz", -1.0
    )
    real_part, imag_part = transform(
        real_part, imag_part, cosine_table.T, sine_table.T, "pkqz,qy->pkyz", -1.0
    )
    packed = jnp.stack((real_part, imag_part), 1).reshape(
        pair_count, 2, width_x, count_y, rows_y, count_z, rows_z
    )
    packed = packed.transpose(0, 1, 3, 5, 4, 6, 2).reshape(
        pair_count, 2, spread * rows_y * rows_z, width_x
    )
    arrived = lax.all_to_all(packed, ("gy", "gz"), split_axis=2, concat_axis=3, tiled=True).reshape(
        pair_count, 2, rows_y, rows_z, period
    )
    return last_section(arrived[:, 0], arrived[:, 1], cosine_table, sine_table, period)


def pad_pairs(values, target):
    extra = target - values.shape[0]
    if extra == 0:
        return values
    widths = [(0, extra)] + [(0, 0)] * (values.ndim - 1)
    return jnp.pad(values, widths)


def shards(i_coeff, j_coeff, pair_orbital, pair_occ):
    fields = jnp.concatenate((i_coeff, j_coeff), 0)
    padded = extended(fields, (("gy", 1), ("gz", 2)), 8)
    orbitals = synthesize(padded)
    own_orbital = orbitals[0]
    local_partners = orbitals[1:]
    local_count = local_partners.shape[0]
    wanted = lax.all_gather(pair_orbital, "band", axis=0, tiled=True)
    first_owned = lax.axis_index("band") * local_count
    slots = jnp.zeros(wanted.shape + own_orbital.shape, jnp.float32)
    for number in range(local_count):
        hit = (wanted == first_owned + number)[:, :, None, None, None]
        slots = jnp.where(hit, local_partners[number][None, None], slots)
    partner = lax.psum_scatter(slots, "band", scatter_dimension=0, tiled=True)[0]
    density = own_orbital[None] * partner
    weights = pair_occ[0].astype(jnp.float32)
    pair_count = density.shape[0]
    group_size = 2
    padded_count = (pair_count + group_size - 1) // group_size * group_size
    density = pad_pairs(density, padded_count)
    partner = pad_pairs(partner, padded_count)
    weights = pad_pairs(weights, padded_count)

    def potentials(density_block):
        block_count = density_block.shape[0]
        density_pairs = density_block.reshape((block_count // 2, 2) + density_block.shape[1:])
        result_real, result_imag = slab_potential(density_pairs[:, 0], density_pairs[:, 1])
        return jnp.stack((result_real, result_imag), 1).reshape(density_block.shape)

    def one_group(number, state_pair):
        applied_now, energy_now = state_pair
        start = number * group_size
        density_one = lax.dynamic_slice_in_dim(density, start, group_size, 0)
        partner_one = lax.dynamic_slice_in_dim(partner, start, group_size, 0)
        weight_one = lax.dynamic_slice_in_dim(weights, start, group_size, 0)
        potential_one = potentials(density_one)
        applied_now = applied_now - jnp.sum(
            weight_one[:, None, None, None] * potential_one * partner_one, axis=0
        )
        energy_now = lax.dynamic_update_slice_in_dim(
            energy_now, jnp.sum(density_one * potential_one, axis=(1, 2, 3)), start, 0
        )
        return (applied_now, energy_now)

    start_state = (
        jnp.zeros(own_orbital.shape, jnp.float32),
        jnp.zeros((padded_count,), jnp.float32),
    )
    applied, local_energy = lax.fori_loop(0, padded_count // group_size, one_group, start_state)
    local_energy = local_energy[:pair_count]
    length = own_orbital.shape[2]
    energy = lax.psum(local_energy, ("gy", "gz")) / float(length**3)
    return (applied[None], energy[None])


def solution(mesh):
    in_specs = (
        P("band", "gy", "gz", None),
        P("band", "gy", "gz", None),
        P("band", None),
        P("band", None),
    )
    out_specs = (P("band", "gy", "gz", None), P("band", None))
    return jax.shard_map(shards, mesh=mesh, in_specs=in_specs, out_specs=out_specs, check_vma=False)
```

```python
import math

import jax
import jax.numpy as jnp
import numpy as np
from jax import lax
from jax.sharding import PartitionSpec as P

tap_offsets = np.arange(-8, 8)
raw_taps = 0.6 ** np.abs(tap_offsets + 0.5) * np.where(tap_offsets % 2 == 0, 1.0, -0.6)
FILTER_TAPS = raw_taps / np.sqrt(np.sum(raw_taps**2))
SCREEN = 0.001
precise_mode = lax.Precision.HIGHEST
fast_mode = lax.Precision.HIGH


def extended(cells, sides, width):
    for axis, dim in sides:
        count = lax.axis_size(axis)
        ends = count - 1
        head = lax.slice_in_dim(cells, 0, width, axis=dim)
        tail = lax.slice_in_dim(cells, cells.shape[dim] - width, cells.shape[dim], axis=dim)
        cells = jnp.concatenate(
            [
                lax.ppermute(tail, axis, [(i, (i + 1) % count) for i in range(ends)]),
                cells,
                lax.ppermute(head, axis, [((i + 1) % count, i) for i in range(ends)]),
            ],
            axis=dim,
        )
    return cells


def band_matrix(row_count, col_count, shift_by):
    row_index = jnp.arange(row_count, dtype=jnp.int32)[:, None]
    col_index = jnp.arange(col_count, dtype=jnp.int32)[None, :]
    offset = row_index - shift_by - col_index
    picked = jnp.zeros((row_count, col_count), jnp.float32)
    for number in range(16):
        picked = picked + jnp.where(offset == number - 8, float(FILTER_TAPS[number]), 0.0)
    return picked


def synthesize(padded):
    wide_y, wide_z, length = (padded.shape[1], padded.shape[2], padded.shape[3])
    matrix_y = band_matrix(wide_y, wide_y - 16, 8)
    matrix_z = band_matrix(wide_z, wide_z - 16, 8)
    matrix_x = band_matrix(length, length, 0)
    step_one = jnp.einsum("oqzx,qy->oyzx", padded, matrix_y, precision=precise_mode)
    step_two = jnp.einsum("oyqx,qz->oyzx", step_one, matrix_z, precision=precise_mode)
    return jnp.matmul(step_two, matrix_x, precision=precise_mode)


def channel_of(channel, length):
    period = 2 * length
    frequency = jnp.where(channel <= length, channel, channel - length)
    angles = 2.0 * math.pi / period * (frequency % period).astype(jnp.float32)
    lattice = 2.0 - 2.0 * jnp.cos(angles)
    fold = jnp.where((channel == 0) | (channel == length), 1.0, 2.0)
    return frequency, lattice, fold


def channel_table(length):
    period = 2 * length
    channel = jnp.arange(period, dtype=jnp.int32)[None, :]
    frequency, _, _ = channel_of(channel, length)
    positions = jnp.arange(length, dtype=jnp.int32)[:, None] * frequency
    angles = 2.0 * math.pi / period * (positions % period).astype(jnp.float32)
    return jnp.where(channel <= length, jnp.cos(angles), jnp.sin(angles))


def contract(left, right, left_dim, right_dim):
    return lax.dot_general(
        left, right, (((left_dim,), (right_dim,)), ((), ())), precision=fast_mode
    )


def potentials(density):
    pair_count, rows_y, rows_z, length = density.shape
    period = 2 * length
    count_y = lax.axis_size("gy")
    count_z = lax.axis_size("gz")
    spread = count_y * count_z
    width = period // spread
    table = channel_table(length)
    flat = density.reshape(pair_count * rows_y * rows_z, length)
    along_x = contract(table, flat, 0, 1)
    send = along_x.reshape(spread, width, pair_count, rows_y * rows_z)
    got = lax.all_to_all(send, ("gy", "gz"), 0, 0, tiled=True)
    got = got.reshape(count_y, count_z, width, pair_count, rows_y, rows_z)
    got = got.transpose(2, 3, 0, 4, 1, 5).reshape(
        width, pair_count, count_y * rows_y, count_z * rows_z
    )
    along_z = contract(got, table, 3, 0)
    spectrum = contract(along_z, table, 2, 0)
    own = lax.axis_index(("gy", "gz")) * width + jnp.arange(width, dtype=jnp.int32)
    _, lattice_x, fold_x = channel_of(own, length)
    _, lattice_all, fold_all = channel_of(jnp.arange(period, dtype=jnp.int32), length)
    weight = (
        fold_x[:, None, None] * fold_all[None, :, None] * fold_all[None, None, :]
    ) / (
        (lattice_x[:, None, None] + lattice_all[None, :, None] + lattice_all[None, None, :] + SCREEN)
        * float(period**3)
    )
    weighted = spectrum * weight[:, None]
    energy_part = jnp.sum(weighted * spectrum, axis=(0, 2, 3))
    back_y = contract(weighted, table, 3, 1)
    back_z = contract(back_y, table, 2, 1)
    back = back_z.reshape(width, pair_count, count_y, rows_y, count_z, rows_z)
    back = back.transpose(2, 4, 0, 1, 3, 5).reshape(spread, width, pair_count, rows_y * rows_z)
    got = lax.all_to_all(back, ("gy", "gz"), 0, 0, tiled=True)
    got = got.reshape(period, pair_count, rows_y * rows_z)
    result = contract(got, table, 0, 1)
    return result.reshape(pair_count, rows_y, rows_z, length), energy_part


def shards(i_coeff, j_coeff, pair_orbital, pair_occ):
    fields = jnp.concatenate((i_coeff, j_coeff), 0)
    padded = extended(fields, (("gy", 1), ("gz", 2)), 8)
    orbitals = synthesize(padded)
    own_orbital = orbitals[0]
    local_partners = orbitals[1:]
    local_count = local_partners.shape[0]
    wanted = lax.all_gather(pair_orbital, "band", axis=0, tiled=True)
    first_owned = lax.axis_index("band") * local_count
    slots = jnp.zeros(wanted.shape + own_orbital.shape, jnp.float32)
    for number in range(local_count):
        hit = (wanted == first_owned + number)[:, :, None, None, None]
        slots = jnp.where(hit, local_partners[number][None, None], slots)
    partner = lax.psum_scatter(slots, "band", scatter_dimension=0, tiled=True)[0]
    density = own_orbital[None] * partner
    potential, energy_part = potentials(density)
    weights = pair_occ[0].astype(jnp.float32)
    applied = -jnp.sum(weights[:, None, None, None] * potential * partner, axis=0)
    length = own_orbital.shape[2]
    energy = lax.psum(energy_part, ("gy", "gz")) / float(length**3)
    return (applied[None], energy[None])


def solution(mesh):
    in_specs = (
        P("band", "gy", "gz", None),
        P("band", "gy", "gz", None),
        P("band", None),
        P("band", None),
    )
    out_specs = (P("band", "gy", "gz", None), P("band", None))
    return jax.shard_map(shards, mesh=mesh, in_specs=in_specs, out_specs=out_specs, check_vma=False)
```

```python
import math

import jax
import jax.numpy as jnp
import numpy as np
from jax import lax
from jax.sharding import PartitionSpec as P

tap_offsets = np.arange(-8, 8)
raw_taps = 0.6 ** np.abs(tap_offsets + 0.5) * np.where(tap_offsets % 2 == 0, 1.0, -0.6)
FILTER_TAPS = raw_taps / np.sqrt(np.sum(raw_taps**2))
SCREEN = 0.001
precise_mode = lax.Precision.HIGHEST
fast_mode = lax.Precision.HIGH


def extended(cells, sides, width):
    for axis, dim in sides:
        count = lax.axis_size(axis)
        ends = count - 1
        head = lax.slice_in_dim(cells, 0, width, axis=dim)
        tail = lax.slice_in_dim(cells, cells.shape[dim] - width, cells.shape[dim], axis=dim)
        cells = jnp.concatenate(
            [
                lax.ppermute(tail, axis, [(i, (i + 1) % count) for i in range(ends)]),
                cells,
                lax.ppermute(head, axis, [((i + 1) % count, i) for i in range(ends)]),
            ],
            axis=dim,
        )
    return cells


def group_sum(values, axes):
    total = values
    for axis in axes:
        count = lax.axis_size(axis)
        if count & (count - 1):
            total = lax.psum(total, axis)
            continue
        step = 1
        while step < count:
            total = total + lax.ppermute(total, axis, [(i, i ^ step) for i in range(count)])
            step *= 2
    return total


def band_matrix(row_count, col_count, shift_by):
    row_index = jnp.arange(row_count, dtype=jnp.int32)[:, None]
    col_index = jnp.arange(col_count, dtype=jnp.int32)[None, :]
    offset = row_index - shift_by - col_index
    picked = jnp.zeros((row_count, col_count), jnp.float32)
    for number in range(16):
        picked = picked + jnp.where(offset == number - 8, float(FILTER_TAPS[number]), 0.0)
    return picked


def synthesize(padded):
    wide_y, wide_z, length = (padded.shape[1], padded.shape[2], padded.shape[3])
    matrix_y = band_matrix(wide_y, wide_y - 16, 8)
    matrix_z = band_matrix(wide_z, wide_z - 16, 8)
    matrix_x = band_matrix(length, length, 0)
    step_one = jnp.einsum("oqzx,qy->oyzx", padded, matrix_y, precision=fast_mode)
    step_two = jnp.einsum("oyqx,qz->oyzx", step_one, matrix_z, precision=fast_mode)
    return jnp.matmul(step_two, matrix_x, precision=fast_mode)


def channel_of(channel, length):
    period = 2 * length
    frequency = jnp.where(channel <= length, channel, channel - length)
    angles = 2.0 * math.pi / period * (frequency % period).astype(jnp.float32)
    lattice = 2.0 - 2.0 * jnp.cos(angles)
    fold = jnp.where((channel == 0) | (channel == length), 1.0, 2.0)
    return frequency, lattice, fold


def channel_table(length):
    period = 2 * length
    channel = jnp.arange(period, dtype=jnp.int32)[None, :]
    frequency, _, _ = channel_of(channel, length)
    positions = jnp.arange(length, dtype=jnp.int32)[:, None] * frequency
    angles = 2.0 * math.pi / period * (positions % period).astype(jnp.float32)
    return jnp.where(channel <= length, jnp.cos(angles), jnp.sin(angles))


def contract(left, right, left_dim, right_dim):
    return lax.dot_general(
        left, right, (((left_dim,), (right_dim,)), ((), ())), precision=fast_mode
    )


def potentials(density):
    pair_count, rows_y, rows_z, length = density.shape
    period = 2 * length
    count_y = lax.axis_size("gy")
    count_z = lax.axis_size("gz")
    spread = count_y * count_z
    width = period // spread
    table = channel_table(length)
    flat = density.reshape(pair_count * rows_y * rows_z, length)
    along_x = contract(table, flat, 0, 1)
    send = along_x.reshape(spread, width, pair_count, rows_y * rows_z)
    got = lax.all_to_all(send, ("gy", "gz"), 0, 0, tiled=True)
    got = got.reshape(count_y, count_z, width, pair_count, rows_y, rows_z)
    got = got.transpose(2, 3, 0, 4, 1, 5).reshape(
        width, pair_count, count_y * rows_y, count_z * rows_z
    )
    along_z = contract(got, table, 3, 0)
    spectrum = contract(along_z, table, 2, 0)
    own = lax.axis_index(("gy", "gz")) * width + jnp.arange(width, dtype=jnp.int32)
    _, lattice_x, fold_x = channel_of(own, length)
    _, lattice_all, fold_all = channel_of(jnp.arange(period, dtype=jnp.int32), length)
    weight = (
        fold_x[:, None, None] * fold_all[None, :, None] * fold_all[None, None, :]
    ) / (
        (lattice_x[:, None, None] + lattice_all[None, :, None] + lattice_all[None, None, :] + SCREEN)
        * float(period**3)
    )
    weighted = spectrum * weight[:, None]
    energy_part = jnp.sum(weighted * spectrum, axis=(0, 2, 3))
    back_y = contract(weighted, table, 3, 1)
    back_z = contract(back_y, table, 2, 1)
    back = back_z.reshape(width, pair_count, count_y, rows_y, count_z, rows_z)
    back = back.transpose(2, 4, 0, 1, 3, 5).reshape(spread, width, pair_count, rows_y * rows_z)
    got = lax.all_to_all(back, ("gy", "gz"), 0, 0, tiled=True)
    got = got.reshape(period, pair_count, rows_y * rows_z)
    result = contract(got, table, 0, 1)
    return result.reshape(pair_count, rows_y, rows_z, length), energy_part


def shards(i_coeff, j_coeff, pair_orbital, pair_occ):
    fields = jnp.concatenate((i_coeff, j_coeff), 0)
    padded = extended(fields, (("gy", 1), ("gz", 2)), 8)
    orbitals = synthesize(padded)
    own_orbital = orbitals[0]
    local_partners = orbitals[1:]
    local_count = local_partners.shape[0]
    band_count = lax.axis_size("band")
    mine = lax.axis_index("band") == jnp.arange(band_count, dtype=jnp.int32)[:, None]
    wanted = group_sum(jnp.where(mine, pair_orbital, 0), ("band",))
    first_owned = lax.axis_index("band") * local_count
    slots = jnp.zeros(wanted.shape + own_orbital.shape, jnp.float32)
    for number in range(local_count):
        hit = (wanted == first_owned + number)[:, :, None, None, None]
        slots = jnp.where(hit, local_partners[number][None, None], slots)
    partner = lax.psum_scatter(slots, "band", scatter_dimension=0, tiled=True)[0]
    density = own_orbital[None] * partner
    potential, energy_part = potentials(density)
    weights = pair_occ[0].astype(jnp.float32)
    applied = -jnp.sum(weights[:, None, None, None] * potential * partner, axis=0)
    length = own_orbital.shape[2]
    energy = group_sum(energy_part, ("gz", "gy")) / float(length**3)
    return (applied[None], energy[None])


def solution(mesh):
    in_specs = (
        P("band", "gy", "gz", None),
        P("band", "gy", "gz", None),
        P("band", None),
        P("band", None),
    )
    out_specs = (P("band", "gy", "gz", None), P("band", None))
    return jax.shard_map(shards, mesh=mesh, in_specs=in_specs, out_specs=out_specs, check_vma=False)
```

```python
import math

import jax
import jax.numpy as jnp
import numpy as np
from jax import lax
from jax.sharding import PartitionSpec as P

tap_offsets = np.arange(-8, 8)
raw_taps = 0.6 ** np.abs(tap_offsets + 0.5) * np.where(tap_offsets % 2 == 0, 1.0, -0.6)
FILTER_TAPS = raw_taps / np.sqrt(np.sum(raw_taps**2))
SCREEN = 0.001
precise_mode = lax.Precision.HIGHEST
fast_mode = lax.Precision.HIGH


def extended(cells, width):
    count_y = lax.axis_size("gy")
    count_z = lax.axis_size("gz")
    rows_y, rows_z = cells.shape[1], cells.shape[2]
    pieces_y = (
        lax.slice_in_dim(cells, rows_y - width, rows_y, axis=1),
        cells,
        lax.slice_in_dim(cells, 0, width, axis=1),
    )
    grid = []
    for shift_y in (-1, 0, 1):
        row = []
        for shift_z in (-1, 0, 1):
            block = pieces_y[shift_y + 1]
            block = (
                lax.slice_in_dim(block, rows_z - width, rows_z, axis=2),
                block,
                lax.slice_in_dim(block, 0, width, axis=2),
            )[shift_z + 1]
            if shift_y == 0 and shift_z == 0:
                row.append(block)
                continue
            pairs = []
            for source_y in range(count_y):
                for source_z in range(count_z):
                    target_y = source_y - shift_y
                    target_z = source_z - shift_z
                    if 0 <= target_y < count_y and 0 <= target_z < count_z:
                        pairs.append((source_y * count_z + source_z, target_y * count_z + target_z))
            row.append(lax.ppermute(block, ("gy", "gz"), pairs))
        grid.append(jnp.concatenate(row, axis=2))
    return jnp.concatenate(grid, axis=1)


def group_sum(values, axes):
    total = values
    for axis in axes:
        count = lax.axis_size(axis)
        if count & (count - 1):
            total = lax.psum(total, axis)
            continue
        step = 1
        while step < count:
            total = total + lax.ppermute(total, axis, [(i, i ^ step) for i in range(count)])
            step *= 2
    return total


def band_matrix(row_count, col_count, shift_by):
    row_index = jnp.arange(row_count, dtype=jnp.int32)[:, None]
    col_index = jnp.arange(col_count, dtype=jnp.int32)[None, :]
    offset = row_index - shift_by - col_index
    picked = jnp.zeros((row_count, col_count), jnp.float32)
    for number in range(16):
        picked = picked + jnp.where(offset == number - 8, float(FILTER_TAPS[number]), 0.0)
    return picked


def synthesize(padded):
    wide_y, wide_z, length = (padded.shape[1], padded.shape[2], padded.shape[3])
    matrix_y = band_matrix(wide_y, wide_y - 16, 8)
    matrix_z = band_matrix(wide_z, wide_z - 16, 8)
    matrix_x = band_matrix(length, length, 0)
    step_one = jnp.einsum("oqzx,qy->oyzx", padded, matrix_y, precision=precise_mode)
    step_two = jnp.einsum("oyqx,qz->oyzx", step_one, matrix_z, precision=precise_mode)
    return jnp.matmul(step_two, matrix_x, precision=precise_mode)


def channel_of(channel, length):
    period = 2 * length
    frequency = jnp.where(channel <= length, channel, channel - length)
    angles = 2.0 * math.pi / period * (frequency % period).astype(jnp.float32)
    lattice = 2.0 - 2.0 * jnp.cos(angles)
    fold = jnp.where((channel == 0) | (channel == length), 1.0, 2.0)
    return frequency, lattice, fold


def channel_table(length):
    period = 2 * length
    channel = jnp.arange(period, dtype=jnp.int32)[None, :]
    frequency, _, _ = channel_of(channel, length)
    positions = jnp.arange(length, dtype=jnp.int32)[:, None] * frequency
    angles = 2.0 * math.pi / period * (positions % period).astype(jnp.float32)
    return jnp.where(channel <= length, jnp.cos(angles), jnp.sin(angles))


def contract(left, right, left_dim, right_dim):
    return lax.dot_general(
        left, right, (((left_dim,), (right_dim,)), ((), ())), precision=fast_mode
    )


def potentials(density):
    pair_count, rows_y, rows_z, length = density.shape
    period = 2 * length
    count_y = lax.axis_size("gy")
    count_z = lax.axis_size("gz")
    spread = count_y * count_z
    width = period // spread
    table = channel_table(length)
    flat = density.reshape(pair_count * rows_y * rows_z, length)
    along_x = contract(table, flat, 0, 1)
    send = along_x.reshape(spread, width, pair_count, rows_y * rows_z)
    got = lax.all_to_all(send, ("gy", "gz"), 0, 0, tiled=True)
    got = got.reshape(count_y, count_z, width, pair_count, rows_y, rows_z)
    got = got.transpose(2, 3, 0, 4, 1, 5).reshape(
        width, pair_count, count_y * rows_y, count_z * rows_z
    )
    along_z = contract(got, table, 3, 0)
    spectrum = contract(along_z, table, 2, 0)
    own = lax.axis_index(("gy", "gz")) * width + jnp.arange(width, dtype=jnp.int32)
    _, lattice_x, fold_x = channel_of(own, length)
    _, lattice_all, fold_all = channel_of(jnp.arange(period, dtype=jnp.int32), length)
    weight = (
        fold_x[:, None, None] * fold_all[None, :, None] * fold_all[None, None, :]
    ) / (
        (lattice_x[:, None, None] + lattice_all[None, :, None] + lattice_all[None, None, :] + SCREEN)
        * float(period**3)
    )
    weighted = spectrum * weight[:, None]
    energy_part = jnp.sum(weighted * spectrum, axis=(0, 2, 3))
    back_y = contract(weighted, table, 3, 1)
    back_z = contract(back_y, table, 2, 1)
    back = back_z.reshape(width, pair_count, count_y, rows_y, count_z, rows_z)
    back = back.transpose(2, 4, 0, 1, 3, 5).reshape(spread, width, pair_count, rows_y * rows_z)
    rider = jnp.broadcast_to(energy_part[None, None, :, None], (spread, width, pair_count, 128))
    back = jnp.concatenate((back, rider), axis=3)
    got = lax.all_to_all(back, ("gy", "gz"), 0, 0, tiled=True)
    energy_total = jnp.sum(got[:, 0, :, rows_y * rows_z], axis=0)
    got = got[:, :, :, : rows_y * rows_z].reshape(period, pair_count, rows_y * rows_z)
    result = contract(got, table, 0, 1)
    return result.reshape(pair_count, rows_y, rows_z, length), energy_total


def shards(i_coeff, j_coeff, pair_orbital, pair_occ):
    local_partners = synthesize(extended(j_coeff, 8))
    local_count = local_partners.shape[0]
    band_count = lax.axis_size("band")
    mine = lax.axis_index("band") == jnp.arange(band_count, dtype=jnp.int32)[:, None]
    wanted = group_sum(jnp.where(mine, pair_orbital, 0), ("band",))
    first_owned = lax.axis_index("band") * local_count
    slots = jnp.zeros(wanted.shape + local_partners.shape[1:], jnp.float32)
    for number in range(local_count):
        hit = (wanted == first_owned + number)[:, :, None, None, None]
        slots = jnp.where(hit, local_partners[number][None, None], slots)
    partner = lax.psum_scatter(slots, "band", scatter_dimension=0, tiled=True)[0]
    own_orbital = synthesize(extended(i_coeff, 8))[0]
    density = own_orbital[None] * partner
    potential, energy_part = potentials(density)
    weights = pair_occ[0].astype(jnp.float32)
    applied = -jnp.sum(weights[:, None, None, None] * potential * partner, axis=0)
    length = own_orbital.shape[2]
    energy = energy_part / float(length**3)
    return (applied[None], energy[None])


def solution(mesh):
    in_specs = (
        P("band", "gy", "gz", None),
        P("band", "gy", "gz", None),
        P("band", None),
        P("band", None),
    )
    out_specs = (P("band", "gy", "gz", None), P("band", None))
    return jax.shard_map(shards, mesh=mesh, in_specs=in_specs, out_specs=out_specs, check_vma=False)
```

```python
import math

import jax
import jax.numpy as jnp
import numpy as np
from jax import lax
from jax.sharding import PartitionSpec as P

tap_offsets = np.arange(-8, 8)
raw_taps = 0.6 ** np.abs(tap_offsets + 0.5) * np.where(tap_offsets % 2 == 0, 1.0, -0.6)
FILTER_TAPS = raw_taps / np.sqrt(np.sum(raw_taps**2))
SCREEN = 0.001
precise_mode = lax.Precision.HIGHEST
fast_mode = lax.Precision.HIGH


def extended(cells, sides, width):
    for axis, dim in sides:
        count = lax.axis_size(axis)
        extent = cells.shape[dim]
        head = lax.slice_in_dim(cells, 0, width, axis=dim)
        tail = lax.slice_in_dim(cells, extent - width, extent, axis=dim)
        if count == 2:
            first = lax.axis_index(axis) == 0
            got = lax.ppermute(jnp.where(first, tail, head), axis, [(0, 1), (1, 0)])
            empty = jnp.zeros_like(got)
            before = jnp.where(first, empty, got)
            after = jnp.where(first, got, empty)
        else:
            before = lax.ppermute(tail, axis, [(i, i + 1) for i in range(count - 1)])
            after = lax.ppermute(head, axis, [(i + 1, i) for i in range(count - 1)])
        cells = jnp.concatenate([before, cells, after], axis=dim)
    return cells


def group_sum(values, axes):
    total = values
    for axis in axes:
        count = lax.axis_size(axis)
        if count & (count - 1):
            total = lax.psum(total, axis)
            continue
        step = 1
        while step < count:
            total = total + lax.ppermute(total, axis, [(i, i ^ step) for i in range(count)])
            step *= 2
    return total


def band_matrix(row_count, col_count, shift_by):
    row_index = jnp.arange(row_count, dtype=jnp.int32)[:, None]
    col_index = jnp.arange(col_count, dtype=jnp.int32)[None, :]
    offset = row_index - shift_by - col_index
    picked = jnp.zeros((row_count, col_count), jnp.float32)
    for number in range(16):
        picked = picked + jnp.where(offset == number - 8, float(FILTER_TAPS[number]), 0.0)
    return picked


def synthesize(padded):
    wide_y, wide_z, length = (padded.shape[1], padded.shape[2], padded.shape[3])
    matrix_y = band_matrix(wide_y, wide_y - 16, 8)
    matrix_z = band_matrix(wide_z, wide_z - 16, 8)
    matrix_x = band_matrix(length, length, 0)
    step_one = jnp.einsum("oqzx,qy->oyzx", padded, matrix_y, precision=precise_mode)
    step_two = jnp.einsum("oyqx,qz->oyzx", step_one, matrix_z, precision=precise_mode)
    return jnp.matmul(step_two, matrix_x, precision=precise_mode)


def channel_of(channel, length):
    period = 2 * length
    frequency = jnp.where(channel <= length, channel, channel - length)
    angles = 2.0 * math.pi / period * (frequency % period).astype(jnp.float32)
    lattice = 2.0 - 2.0 * jnp.cos(angles)
    fold = jnp.where((channel == 0) | (channel == length), 1.0, 2.0)
    return frequency, lattice, fold


def channel_table(length):
    period = 2 * length
    channel = jnp.arange(period, dtype=jnp.int32)[None, :]
    frequency, _, _ = channel_of(channel, length)
    positions = jnp.arange(length, dtype=jnp.int32)[:, None] * frequency
    angles = 2.0 * math.pi / period * (positions % period).astype(jnp.float32)
    return jnp.where(channel <= length, jnp.cos(angles), jnp.sin(angles))


def contract(left, right, left_dim, right_dim):
    return lax.dot_general(
        left, right, (((left_dim,), (right_dim,)), ((), ())), precision=fast_mode
    )


def potentials(density):
    pair_count, rows_y, rows_z, length = density.shape
    period = 2 * length
    count_y = lax.axis_size("gy")
    count_z = lax.axis_size("gz")
    spread = count_y * count_z
    width = period // spread
    table = channel_table(length)
    flat = density.reshape(pair_count * rows_y * rows_z, length)
    along_x = contract(table, flat, 0, 1)
    send = along_x.reshape(spread, width, pair_count, rows_y * rows_z)
    got = lax.all_to_all(send, ("gy", "gz"), 0, 0, tiled=True)
    got = got.reshape(count_y, count_z, width, pair_count, rows_y, rows_z)
    got = got.transpose(2, 3, 0, 4, 1, 5).reshape(
        width, pair_count, count_y * rows_y, count_z * rows_z
    )
    along_z = contract(got, table, 3, 0)
    spectrum = contract(along_z, table, 2, 0)
    own = lax.axis_index(("gy", "gz")) * width + jnp.arange(width, dtype=jnp.int32)
    _, lattice_x, fold_x = channel_of(own, length)
    _, lattice_all, fold_all = channel_of(jnp.arange(period, dtype=jnp.int32), length)
    weight = (
        fold_x[:, None, None] * fold_all[None, :, None] * fold_all[None, None, :]
    ) / (
        (lattice_x[:, None, None] + lattice_all[None, :, None] + lattice_all[None, None, :] + SCREEN)
        * float(period**3)
    )
    weighted = spectrum * weight[:, None]
    energy_part = jnp.sum(weighted * spectrum, axis=(0, 2, 3))
    back_y = contract(weighted, table, 3, 1)
    back_z = contract(back_y, table, 2, 1)
    back = back_z.reshape(width, pair_count, count_y, rows_y, count_z, rows_z)
    back = back.transpose(2, 4, 0, 1, 3, 5).reshape(spread, width, pair_count, rows_y * rows_z)
    rider = jnp.broadcast_to(energy_part[None, None, :, None], (spread, width, pair_count, 128))
    back = jnp.concatenate((back, rider), axis=3)
    got = lax.all_to_all(back, ("gy", "gz"), 0, 0, tiled=True)
    energy_total = jnp.sum(got[:, 0, :, rows_y * rows_z], axis=0)
    got = got[:, :, :, : rows_y * rows_z].reshape(period, pair_count, rows_y * rows_z)
    result = contract(got, table, 0, 1)
    return result.reshape(pair_count, rows_y, rows_z, length), energy_total


def shards(i_coeff, j_coeff, pair_orbital, pair_occ):
    fields = jnp.concatenate((i_coeff, j_coeff), 0)
    padded = extended(fields, (("gy", 1), ("gz", 2)), 8)
    own_count = i_coeff.shape[0]
    local_partners = synthesize(padded[own_count:])
    local_count = local_partners.shape[0]
    band_count = lax.axis_size("band")
    mine = lax.axis_index("band") == jnp.arange(band_count, dtype=jnp.int32)[:, None]
    wanted = group_sum(jnp.where(mine, pair_orbital, 0), ("band",))
    first_owned = lax.axis_index("band") * local_count
    slots = jnp.zeros(wanted.shape + local_partners.shape[1:], jnp.float32)
    for number in range(local_count):
        hit = (wanted == first_owned + number)[:, :, None, None, None]
        slots = jnp.where(hit, local_partners[number][None, None], slots)
    partner = lax.psum_scatter(slots, "band", scatter_dimension=0, tiled=True)[0]
    own_orbital = synthesize(padded[:own_count])[0]
    density = own_orbital[None] * partner
    potential, energy_part = potentials(density)
    weights = pair_occ[0].astype(jnp.float32)
    applied = -jnp.sum(weights[:, None, None, None] * potential * partner, axis=0)
    length = own_orbital.shape[2]
    energy = energy_part / float(length**3)
    return (applied[None], energy[None])


def solution(mesh):
    in_specs = (
        P("band", "gy", "gz", None),
        P("band", "gy", "gz", None),
        P("band", None),
        P("band", None),
    )
    out_specs = (P("band", "gy", "gz", None), P("band", None))
    return jax.shard_map(shards, mesh=mesh, in_specs=in_specs, out_specs=out_specs, check_vma=False)
```

```python
import math

import jax
import jax.numpy as jnp
import numpy as np
from jax import lax
from jax.sharding import PartitionSpec as P

tap_offsets = np.arange(-8, 8)
raw_taps = 0.6 ** np.abs(tap_offsets + 0.5) * np.where(tap_offsets % 2 == 0, 1.0, -0.6)
FILTER_TAPS = raw_taps / np.sqrt(np.sum(raw_taps**2))
SCREEN = 0.001
precise_mode = lax.Precision.HIGHEST
fast_mode = lax.Precision.HIGH


def extended(cells, sides, width):
    for axis, dim in sides:
        count = lax.axis_size(axis)
        extent = cells.shape[dim]
        head = lax.slice_in_dim(cells, 0, width, axis=dim)
        tail = lax.slice_in_dim(cells, extent - width, extent, axis=dim)
        if count == 2:
            first = lax.axis_index(axis) == 0
            got = lax.ppermute(jnp.where(first, tail, head), axis, [(0, 1), (1, 0)])
            empty = jnp.zeros_like(got)
            before = jnp.where(first, empty, got)
            after = jnp.where(first, got, empty)
        else:
            before = lax.ppermute(tail, axis, [(i, i + 1) for i in range(count - 1)])
            after = lax.ppermute(head, axis, [(i + 1, i) for i in range(count - 1)])
        cells = jnp.concatenate([before, cells, after], axis=dim)
    return cells


def group_sum(values, axes):
    total = values
    for axis in axes:
        count = lax.axis_size(axis)
        if count & (count - 1):
            total = lax.psum(total, axis)
            continue
        step = 1
        while step < count:
            total = total + lax.ppermute(total, axis, [(i, i ^ step) for i in range(count)])
            step *= 2
    return total


def band_matrix(row_count, col_count, shift_by):
    row_index = jnp.arange(row_count, dtype=jnp.int32)[:, None]
    col_index = jnp.arange(col_count, dtype=jnp.int32)[None, :]
    offset = row_index - shift_by - col_index
    picked = jnp.zeros((row_count, col_count), jnp.float32)
    for number in range(16):
        picked = picked + jnp.where(offset == number - 8, float(FILTER_TAPS[number]), 0.0)
    return picked


def synthesize(padded):
    wide_y, wide_z, length = (padded.shape[1], padded.shape[2], padded.shape[3])
    matrix_y = band_matrix(wide_y, wide_y - 16, 8)
    matrix_z = band_matrix(wide_z, wide_z - 16, 8)
    matrix_x = band_matrix(length, length, 0)
    step_one = jnp.einsum("oqzx,qy->oyzx", padded, matrix_y, precision=precise_mode)
    step_two = jnp.einsum("oyqx,qz->oyzx", step_one, matrix_z, precision=precise_mode)
    return jnp.matmul(step_two, matrix_x, precision=precise_mode)


def channel_of(channel, length):
    period = 2 * length
    frequency = jnp.where(channel <= length, channel, channel - length)
    angles = 2.0 * math.pi / period * (frequency % period).astype(jnp.float32)
    lattice = 2.0 - 2.0 * jnp.cos(angles)
    fold = jnp.where((channel == 0) | (channel == length), 1.0, 2.0)
    return frequency, lattice, fold


def channel_table(length):
    period = 2 * length
    channel = jnp.arange(period, dtype=jnp.int32)[None, :]
    frequency, _, _ = channel_of(channel, length)
    positions = jnp.arange(length, dtype=jnp.int32)[:, None] * frequency
    angles = 2.0 * math.pi / period * (positions % period).astype(jnp.float32)
    return jnp.where(channel <= length, jnp.cos(angles), jnp.sin(angles))


def contract(left, right, left_dim, right_dim):
    return lax.dot_general(
        left, right, (((left_dim,), (right_dim,)), ((), ())), precision=fast_mode
    )


def potentials(density):
    pair_count, rows_y, rows_z, length = density.shape
    period = 2 * length
    count_y = lax.axis_size("gy")
    count_z = lax.axis_size("gz")
    spread = count_y * count_z
    width = period // spread
    face = rows_y * rows_z
    table = channel_table(length)
    flat = density.reshape(pair_count * face, length)
    along_x = contract(table, flat, 0, 1)
    send = along_x.reshape(spread, width, pair_count, face)
    stages = 2 if width % 2 == 0 else 1
    piece = width // stages
    _, lattice_all, fold_all = channel_of(jnp.arange(period, dtype=jnp.int32), length)
    inverse_x = table.reshape(length, spread, width)
    result = None
    energy_total = None
    for stage in range(stages):
        part = send[:, stage * piece : (stage + 1) * piece]
        got = lax.all_to_all(part, ("gy", "gz"), 0, 0, tiled=True)
        got = got.reshape(count_y, count_z, piece, pair_count, rows_y, rows_z)
        got = got.transpose(2, 3, 0, 4, 1, 5).reshape(
            piece, pair_count, count_y * rows_y, count_z * rows_z
        )
        along_z = contract(got, table, 3, 0)
        spectrum = contract(along_z, table, 2, 0)
        own = (
            lax.axis_index(("gy", "gz")) * width
            + stage * piece
            + jnp.arange(piece, dtype=jnp.int32)
        )
        _, lattice_x, fold_x = channel_of(own, length)
        weight = (
            fold_x[:, None, None] * fold_all[None, :, None] * fold_all[None, None, :]
        ) / (
            (lattice_x[:, None, None] + lattice_all[None, :, None] + lattice_all[None, None, :] + SCREEN)
            * float(period**3)
        )
        weighted = spectrum * weight[:, None]
        energy_part = jnp.sum(weighted * spectrum, axis=(0, 2, 3))
        back_y = contract(weighted, table, 3, 1)
        back_z = contract(back_y, table, 2, 1)
        back = back_z.reshape(piece, pair_count, count_y, rows_y, count_z, rows_z)
        back = back.transpose(2, 4, 0, 1, 3, 5).reshape(spread, piece, pair_count, face)
        rider = jnp.broadcast_to(energy_part[None, None, :, None], (spread, piece, pair_count, 128))
        back = jnp.concatenate((back, rider), axis=3)
        got = lax.all_to_all(back, ("gy", "gz"), 0, 0, tiled=True)
        energy_here = jnp.sum(got[:, 0, :, face], axis=0)
        columns = inverse_x[:, :, stage * piece : (stage + 1) * piece]
        contribution = lax.dot_general(
            got[:, :, :, :face], columns, (((0, 1), (1, 2)), ((), ())), precision=fast_mode
        )
        result = contribution if result is None else result + contribution
        energy_total = energy_here if energy_total is None else energy_total + energy_here
    return result.reshape(pair_count, rows_y, rows_z, length), energy_total


def shards(i_coeff, j_coeff, pair_orbital, pair_occ):
    fields = jnp.concatenate((i_coeff, j_coeff), 0)
    padded = extended(fields, (("gy", 1), ("gz", 2)), 8)
    own_count = i_coeff.shape[0]
    local_partners = synthesize(padded[own_count:])
    local_count = local_partners.shape[0]
    band_count = lax.axis_size("band")
    mine = lax.axis_index("band") == jnp.arange(band_count, dtype=jnp.int32)[:, None]
    wanted = group_sum(jnp.where(mine, pair_orbital, 0), ("band",))
    first_owned = lax.axis_index("band") * local_count
    slots = jnp.zeros(wanted.shape + local_partners.shape[1:], jnp.float32)
    for number in range(local_count):
        hit = (wanted == first_owned + number)[:, :, None, None, None]
        slots = jnp.where(hit, local_partners[number][None, None], slots)
    partner = lax.psum_scatter(slots, "band", scatter_dimension=0, tiled=True)[0]
    own_orbital = synthesize(padded[:own_count])[0]
    density = own_orbital[None] * partner
    potential, energy_part = potentials(density)
    weights = pair_occ[0].astype(jnp.float32)
    applied = -jnp.sum(weights[:, None, None, None] * potential * partner, axis=0)
    length = own_orbital.shape[2]
    energy = energy_part / float(length**3)
    return (applied[None], energy[None])


def solution(mesh):
    in_specs = (
        P("band", "gy", "gz", None),
        P("band", "gy", "gz", None),
        P("band", None),
        P("band", None),
    )
    out_specs = (P("band", "gy", "gz", None), P("band", None))
    return jax.shard_map(shards, mesh=mesh, in_specs=in_specs, out_specs=out_specs, check_vma=False)
```

```python
import math

import jax
import jax.numpy as jnp
import numpy as np
from jax import lax
from jax.sharding import PartitionSpec as P

tap_offsets = np.arange(-8, 8)
raw_taps = 0.6 ** np.abs(tap_offsets + 0.5) * np.where(tap_offsets % 2 == 0, 1.0, -0.6)
FILTER_TAPS = raw_taps / np.sqrt(np.sum(raw_taps**2))
SCREEN = 0.001
precise_mode = lax.Precision.HIGHEST
fast_mode = lax.Precision.HIGH


def extended(cells, sides, width):
    for axis, dim in sides:
        count = lax.axis_size(axis)
        extent = cells.shape[dim]
        head = lax.slice_in_dim(cells, 0, width, axis=dim)
        tail = lax.slice_in_dim(cells, extent - width, extent, axis=dim)
        if count == 2:
            first = lax.axis_index(axis) == 0
            got = lax.ppermute(jnp.where(first, tail, head), axis, [(0, 1), (1, 0)])
            empty = jnp.zeros_like(got)
            before = jnp.where(first, empty, got)
            after = jnp.where(first, got, empty)
        else:
            before = lax.ppermute(tail, axis, [(i, i + 1) for i in range(count - 1)])
            after = lax.ppermute(head, axis, [(i + 1, i) for i in range(count - 1)])
        cells = jnp.concatenate([before, cells, after], axis=dim)
    return cells


def group_sum(values, axes):
    total = values
    for axis in axes:
        count = lax.axis_size(axis)
        if count & (count - 1):
            total = lax.psum(total, axis)
            continue
        step = 1
        while step < count:
            total = total + lax.ppermute(total, axis, [(i, i ^ step) for i in range(count)])
            step *= 2
    return total


def band_matrix(row_count, col_count, shift_by):
    row_index = jnp.arange(row_count, dtype=jnp.int32)[:, None]
    col_index = jnp.arange(col_count, dtype=jnp.int32)[None, :]
    offset = row_index - shift_by - col_index
    picked = jnp.zeros((row_count, col_count), jnp.float32)
    for number in range(16):
        picked = picked + jnp.where(offset == number - 8, float(FILTER_TAPS[number]), 0.0)
    return picked


def synthesize(padded):
    wide_y, wide_z, length = (padded.shape[1], padded.shape[2], padded.shape[3])
    matrix_y = band_matrix(wide_y, wide_y - 16, 8)
    matrix_z = band_matrix(wide_z, wide_z - 16, 8)
    matrix_x = band_matrix(length, length, 0)
    step_one = jnp.matmul(padded, matrix_x, precision=precise_mode)
    step_two = jnp.einsum("oyqx,qz->oyzx", step_one, matrix_z, precision=precise_mode)
    return jnp.einsum("oqzx,qy->oyzx", step_two, matrix_y, precision=precise_mode)


def channel_of(channel, length):
    period = 2 * length
    frequency = jnp.where(channel <= length, channel, channel - length)
    angles = 2.0 * math.pi / period * (frequency % period).astype(jnp.float32)
    lattice = 2.0 - 2.0 * jnp.cos(angles)
    fold = jnp.where((channel == 0) | (channel == length), 1.0, 2.0)
    return frequency, lattice, fold


def channel_table(length):
    period = 2 * length
    channel = jnp.arange(period, dtype=jnp.int32)[None, :]
    frequency, _, _ = channel_of(channel, length)
    positions = jnp.arange(length, dtype=jnp.int32)[:, None] * frequency
    angles = 2.0 * math.pi / period * (positions % period).astype(jnp.float32)
    return jnp.where(channel <= length, jnp.cos(angles), jnp.sin(angles))


def contract(left, right, left_dim, right_dim):
    return lax.dot_general(
        left, right, (((left_dim,), (right_dim,)), ((), ())), precision=fast_mode
    )


def potentials(density):
    pair_count, rows_y, rows_z, length = density.shape
    period = 2 * length
    count_y = lax.axis_size("gy")
    count_z = lax.axis_size("gz")
    spread = count_y * count_z
    width = period // spread
    table = channel_table(length)
    flat = density.reshape(pair_count * rows_y * rows_z, length)
    along_x = contract(table, flat, 0, 1)
    send = along_x.reshape(spread, width, pair_count, rows_y * rows_z)
    got = lax.all_to_all(send, ("gy", "gz"), 0, 0, tiled=True)
    got = got.reshape(count_y, count_z, width, pair_count, rows_y, rows_z)
    got = got.transpose(2, 3, 0, 4, 1, 5).reshape(
        width, pair_count, count_y * rows_y, count_z * rows_z
    )
    along_z = contract(got, table, 3, 0)
    spectrum = contract(along_z, table, 2, 0)
    own = lax.axis_index(("gy", "gz")) * width + jnp.arange(width, dtype=jnp.int32)
    _, lattice_x, fold_x = channel_of(own, length)
    _, lattice_all, fold_all = channel_of(jnp.arange(period, dtype=jnp.int32), length)
    weight = (
        fold_x[:, None, None] * fold_all[None, :, None] * fold_all[None, None, :]
    ) / (
        (lattice_x[:, None, None] + lattice_all[None, :, None] + lattice_all[None, None, :] + SCREEN)
        * float(period**3)
    )
    weighted = spectrum * weight[:, None]
    energy_part = jnp.sum(weighted * spectrum, axis=(0, 2, 3))
    back_y = contract(weighted, table, 3, 1)
    back_z = contract(back_y, table, 2, 1)
    back = back_z.reshape(width, pair_count, count_y, rows_y, count_z, rows_z)
    back = back.transpose(2, 4, 0, 1, 3, 5).reshape(spread, width, pair_count, rows_y * rows_z)
    rider = jnp.broadcast_to(energy_part[None, None, :, None], (spread, width, pair_count, 128))
    back = jnp.concatenate((back, rider), axis=3)
    got = lax.all_to_all(back, ("gy", "gz"), 0, 0, tiled=True)
    energy_total = jnp.sum(got[:, 0, :, rows_y * rows_z], axis=0)
    got = got[:, :, :, : rows_y * rows_z].reshape(period, pair_count, rows_y * rows_z)
    result = contract(got, table, 0, 1)
    return result.reshape(pair_count, rows_y, rows_z, length), energy_total


def shards(i_coeff, j_coeff, pair_orbital, pair_occ):
    fields = jnp.concatenate((i_coeff, j_coeff), 0)
    padded = extended(fields, (("gy", 1), ("gz", 2)), 8)
    own_count = i_coeff.shape[0]
    local_partners = synthesize(padded[own_count:])
    local_count = local_partners.shape[0]
    band_count = lax.axis_size("band")
    mine = lax.axis_index("band") == jnp.arange(band_count, dtype=jnp.int32)[:, None]
    wanted = group_sum(jnp.where(mine, pair_orbital, 0), ("band",))
    first_owned = lax.axis_index("band") * local_count
    slots = jnp.zeros(wanted.shape + local_partners.shape[1:], jnp.float32)
    for number in range(local_count):
        hit = (wanted == first_owned + number)[:, :, None, None, None]
        slots = jnp.where(hit, local_partners[number][None, None], slots)
    partner = lax.psum_scatter(slots, "band", scatter_dimension=0, tiled=True)[0]
    own_orbital = synthesize(padded[:own_count])[0]
    density = own_orbital[None] * partner
    potential, energy_part = potentials(density)
    weights = pair_occ[0].astype(jnp.float32)
    applied = -jnp.sum(weights[:, None, None, None] * potential * partner, axis=0)
    length = own_orbital.shape[2]
    energy = energy_part / float(length**3)
    return (applied[None], energy[None])


def solution(mesh):
    in_specs = (
        P("band", "gy", "gz", None),
        P("band", "gy", "gz", None),
        P("band", None),
        P("band", None),
    )
    out_specs = (P("band", "gy", "gz", None), P("band", None))
    return jax.shard_map(shards, mesh=mesh, in_specs=in_specs, out_specs=out_specs, check_vma=False)
```

```python
import math

import jax
import jax.numpy as jnp
import numpy as np
from jax import lax
from jax.sharding import PartitionSpec as P

tap_offsets = np.arange(-8, 8)
raw_taps = 0.6 ** np.abs(tap_offsets + 0.5) * np.where(tap_offsets % 2 == 0, 1.0, -0.6)
FILTER_TAPS = raw_taps / np.sqrt(np.sum(raw_taps**2))
SCREEN = 0.001
precise_mode = lax.Precision.HIGHEST
fast_mode = lax.Precision.HIGH


def extended(cells, sides, width):
    for axis, dim in sides:
        count = lax.axis_size(axis)
        extent = cells.shape[dim]
        head = lax.slice_in_dim(cells, 0, width, axis=dim)
        tail = lax.slice_in_dim(cells, extent - width, extent, axis=dim)
        if count == 2:
            first = lax.axis_index(axis) == 0
            got = lax.ppermute(jnp.where(first, tail, head), axis, [(0, 1), (1, 0)])
            empty = jnp.zeros_like(got)
            before = jnp.where(first, empty, got)
            after = jnp.where(first, got, empty)
        else:
            before = lax.ppermute(tail, axis, [(i, i + 1) for i in range(count - 1)])
            after = lax.ppermute(head, axis, [(i + 1, i) for i in range(count - 1)])
        cells = jnp.concatenate([before, cells, after], axis=dim)
    return cells


def group_sum(values, axes):
    total = values
    for axis in axes:
        count = lax.axis_size(axis)
        if count & (count - 1):
            total = lax.psum(total, axis)
            continue
        step = 1
        while step < count:
            total = total + lax.ppermute(total, axis, [(i, i ^ step) for i in range(count)])
            step *= 2
    return total


def band_matrix(row_count, col_count, shift_by):
    row_index = jnp.arange(row_count, dtype=jnp.int32)[:, None]
    col_index = jnp.arange(col_count, dtype=jnp.int32)[None, :]
    offset = row_index - shift_by - col_index
    picked = jnp.zeros((row_count, col_count), jnp.float32)
    for number in range(16):
        picked = picked + jnp.where(offset == number - 8, float(FILTER_TAPS[number]), 0.0)
    return picked


def synthesize(padded):
    wide_y, wide_z, length = (padded.shape[1], padded.shape[2], padded.shape[3])
    matrix_y = band_matrix(wide_y, wide_y - 16, 8)
    matrix_z = band_matrix(wide_z, wide_z - 16, 8)
    matrix_x = band_matrix(length, length, 0)
    step_one = jnp.matmul(padded, matrix_x, precision=precise_mode)
    step_two = jnp.einsum("oyqx,qz->oyzx", step_one, matrix_z, precision=precise_mode)
    return jnp.einsum("oqzx,qy->oyzx", step_two, matrix_y, precision=precise_mode)


def channel_of(channel, length):
    period = 2 * length
    frequency = jnp.where(channel <= length, channel, channel - length)
    angles = 2.0 * math.pi / period * (frequency % period).astype(jnp.float32)
    lattice = 2.0 - 2.0 * jnp.cos(angles)
    fold = jnp.where((channel == 0) | (channel == length), 1.0, 2.0)
    return frequency, lattice, fold


def channel_table(length):
    period = 2 * length
    channel = jnp.arange(period, dtype=jnp.int32)[None, :]
    frequency, _, _ = channel_of(channel, length)
    positions = jnp.arange(length, dtype=jnp.int32)[:, None] * frequency
    angles = 2.0 * math.pi / period * (positions % period).astype(jnp.float32)
    return jnp.where(channel <= length, jnp.cos(angles), jnp.sin(angles))


def contract(left, right, left_dim, right_dim):
    return lax.dot_general(
        left, right, (((left_dim,), (right_dim,)), ((), ())), precision=fast_mode
    )


def potentials(density):
    pair_count, rows_y, rows_z, length = density.shape
    period = 2 * length
    count_y = lax.axis_size("gy")
    count_z = lax.axis_size("gz")
    spread = count_y * count_z
    width = period // spread
    table = channel_table(length)
    flat = density.reshape(pair_count * rows_y * rows_z, length)
    along_x = contract(table, flat, 0, 1)
    send = along_x.reshape(spread, width, pair_count, rows_y * rows_z)
    got = lax.all_to_all(send, ("gy", "gz"), 0, 0, tiled=True)
    got = got.reshape(count_y, count_z, width, pair_count, rows_y, rows_z)
    got = got.transpose(2, 3, 0, 4, 1, 5).reshape(
        width, pair_count, count_y * rows_y, count_z * rows_z
    )
    along_z = contract(got, table, 3, 0)
    spectrum = contract(along_z, table, 2, 0)
    own = lax.axis_index(("gy", "gz")) * width + jnp.arange(width, dtype=jnp.int32)
    _, lattice_x, fold_x = channel_of(own, length)
    _, lattice_all, fold_all = channel_of(jnp.arange(period, dtype=jnp.int32), length)
    weight = (
        fold_x[:, None, None] * fold_all[None, :, None] * fold_all[None, None, :]
    ) / (
        (lattice_x[:, None, None] + lattice_all[None, :, None] + lattice_all[None, None, :] + SCREEN)
        * float(period**3)
    )
    weighted = spectrum * weight[:, None]
    energy_part = jnp.sum(weighted * spectrum, axis=(0, 2, 3))
    back_y = contract(weighted, table, 3, 1)
    back_z = contract(back_y, table, 2, 1)
    back = back_z.reshape(width, pair_count, count_y, rows_y, count_z, rows_z)
    back = back.transpose(2, 4, 0, 1, 3, 5).reshape(spread, width, pair_count, rows_y * rows_z)
    rider = jnp.broadcast_to(energy_part[None, None, :, None], (spread, width, pair_count, 128))
    back = jnp.concatenate((back, rider), axis=3)
    got = lax.all_to_all(back, ("gy", "gz"), 0, 0, tiled=True)
    energy_total = jnp.sum(got[:, 0, :, rows_y * rows_z], axis=0)
    got = got[:, :, :, : rows_y * rows_z].reshape(period, pair_count, rows_y * rows_z)
    result = contract(got, table, 0, 1)
    return result.reshape(pair_count, rows_y, rows_z, length), energy_total


def shards(i_coeff, j_coeff, pair_orbital, pair_occ):
    fields = jnp.concatenate((i_coeff, j_coeff), 0)
    padded = extended(fields, (("gy", 1), ("gz", 2)), 8)
    own_count = i_coeff.shape[0]
    local_partners = synthesize(padded[own_count:])
    local_count = local_partners.shape[0]
    band_count = lax.axis_size("band")
    mine = lax.axis_index("band") == jnp.arange(band_count, dtype=jnp.int32)[:, None]
    wanted = group_sum(jnp.where(mine, pair_orbital, 0), ("band",))
    first_owned = lax.axis_index("band") * local_count
    slots = jnp.zeros(wanted.shape + local_partners.shape[1:], jnp.float32)
    for number in range(local_count):
        hit = (wanted == first_owned + number)[:, :, None, None, None]
        slots = jnp.where(hit, local_partners[number][None, None], slots)
    partner = jnp.sum(lax.all_to_all(slots, "band", 0, 0, tiled=True), axis=0)
    own_orbital = synthesize(padded[:own_count])[0]
    density = own_orbital[None] * partner
    potential, energy_part = potentials(density)
    weights = pair_occ[0].astype(jnp.float32)
    applied = -jnp.sum(weights[:, None, None, None] * potential * partner, axis=0)
    length = own_orbital.shape[2]
    energy = energy_part / float(length**3)
    return (applied[None], energy[None])


def solution(mesh):
    in_specs = (
        P("band", "gy", "gz", None),
        P("band", "gy", "gz", None),
        P("band", None),
        P("band", None),
    )
    out_specs = (P("band", "gy", "gz", None), P("band", None))
    return jax.shard_map(shards, mesh=mesh, in_specs=in_specs, out_specs=out_specs, check_vma=False)
```

```python
import math

import jax
import jax.numpy as jnp
import numpy as np
from jax import lax
from jax.sharding import PartitionSpec as P

tap_offsets = np.arange(-8, 8)
raw_taps = 0.6 ** np.abs(tap_offsets + 0.5) * np.where(tap_offsets % 2 == 0, 1.0, -0.6)
FILTER_TAPS = raw_taps / np.sqrt(np.sum(raw_taps**2))
SCREEN = 0.001
precise_mode = lax.Precision.HIGHEST
fast_mode = lax.Precision.HIGH


def extended(cells, sides, width):
    for axis, dim in sides:
        count = lax.axis_size(axis)
        extent = cells.shape[dim]
        head = lax.slice_in_dim(cells, 0, width, axis=dim)
        tail = lax.slice_in_dim(cells, extent - width, extent, axis=dim)
        if count == 2:
            first = lax.axis_index(axis) == 0
            got = lax.ppermute(jnp.where(first, tail, head), axis, [(0, 1), (1, 0)])
            empty = jnp.zeros_like(got)
            before = jnp.where(first, empty, got)
            after = jnp.where(first, got, empty)
        else:
            before = lax.ppermute(tail, axis, [(i, i + 1) for i in range(count - 1)])
            after = lax.ppermute(head, axis, [(i + 1, i) for i in range(count - 1)])
        cells = jnp.concatenate([before, cells, after], axis=dim)
    return cells


def group_sum(values, axes):
    total = values
    for axis in axes:
        count = lax.axis_size(axis)
        if count & (count - 1):
            total = lax.psum(total, axis)
            continue
        step = 1
        while step < count:
            total = total + lax.ppermute(total, axis, [(i, i ^ step) for i in range(count)])
            step *= 2
    return total


def band_matrix(row_count, col_count, shift_by):
    row_index = jnp.arange(row_count, dtype=jnp.int32)[:, None]
    col_index = jnp.arange(col_count, dtype=jnp.int32)[None, :]
    offset = row_index - shift_by - col_index
    picked = jnp.zeros((row_count, col_count), jnp.float32)
    for number in range(16):
        picked = picked + jnp.where(offset == number - 8, float(FILTER_TAPS[number]), 0.0)
    return picked


def synthesize(padded):
    wide_y, wide_z, length = (padded.shape[1], padded.shape[2], padded.shape[3])
    matrix_y = band_matrix(wide_y, wide_y - 16, 8)
    matrix_z = band_matrix(wide_z, wide_z - 16, 8)
    matrix_x = band_matrix(length, length, 0)
    step_one = jnp.matmul(padded, matrix_x, precision=precise_mode)
    step_two = jnp.einsum("oyqx,qz->oyzx", step_one, matrix_z, precision=precise_mode)
    return jnp.einsum("oqzx,qy->oyzx", step_two, matrix_y, precision=precise_mode)


def channel_of(channel, length):
    period = 2 * length
    frequency = jnp.where(channel <= length, channel, channel - length)
    angles = 2.0 * math.pi / period * (frequency % period).astype(jnp.float32)
    lattice = 2.0 - 2.0 * jnp.cos(angles)
    fold = jnp.where((channel == 0) | (channel == length), 1.0, 2.0)
    return frequency, lattice, fold


def channel_table(length):
    period = 2 * length
    channel = jnp.arange(period, dtype=jnp.int32)[None, :]
    frequency, _, _ = channel_of(channel, length)
    positions = jnp.arange(length, dtype=jnp.int32)[:, None] * frequency
    angles = 2.0 * math.pi / period * (positions % period).astype(jnp.float32)
    return jnp.where(channel <= length, jnp.cos(angles), jnp.sin(angles))


def contract(left, right, left_dim, right_dim):
    return lax.dot_general(
        left, right, (((left_dim,), (right_dim,)), ((), ())), precision=fast_mode
    )


def potentials(density):
    pair_count, rows_y, rows_z, length = density.shape
    period = 2 * length
    count_y = lax.axis_size("gy")
    count_z = lax.axis_size("gz")
    spread = count_y * count_z
    width = period // spread
    table = channel_table(length)
    flat = density.reshape(pair_count * rows_y * rows_z, length)
    along_x = contract(table, flat, 0, 1)
    send = along_x.reshape(spread, width, pair_count, rows_y * rows_z)
    got = lax.all_to_all(send, ("gy", "gz"), 0, 0, tiled=True)
    got = got.reshape(count_y, count_z, width, pair_count, rows_y, rows_z)
    got = got.transpose(2, 3, 0, 4, 1, 5).reshape(
        width, pair_count, count_y * rows_y, count_z * rows_z
    )
    along_z = contract(got, table, 3, 0)
    spectrum = contract(along_z, table, 2, 0)
    own = lax.axis_index(("gy", "gz")) * width + jnp.arange(width, dtype=jnp.int32)
    _, lattice_x, fold_x = channel_of(own, length)
    _, lattice_all, fold_all = channel_of(jnp.arange(period, dtype=jnp.int32), length)
    weight = (
        fold_x[:, None, None] * fold_all[None, :, None] * fold_all[None, None, :]
    ) / (
        (lattice_x[:, None, None] + lattice_all[None, :, None] + lattice_all[None, None, :] + SCREEN)
        * float(period**3)
    )
    weighted = spectrum * weight[:, None]
    energy_part = jnp.sum(weighted * spectrum, axis=(0, 2, 3))
    back_y = contract(weighted, table, 3, 1)
    back_z = contract(back_y, table, 2, 1)
    back = back_z.reshape(width, pair_count, count_y, rows_y, count_z, rows_z)
    back = back.transpose(2, 4, 0, 1, 3, 5).reshape(spread, width, pair_count, rows_y * rows_z)
    rider = jnp.broadcast_to(energy_part[None, None, :, None], (spread, width, pair_count, 128))
    back = jnp.concatenate((back, rider), axis=3)
    got = lax.all_to_all(back, ("gy", "gz"), 0, 0, tiled=True)
    energy_total = jnp.sum(got[:, 0, :, rows_y * rows_z], axis=0)
    got = got[:, :, :, : rows_y * rows_z].reshape(period, pair_count, rows_y * rows_z)
    result = contract(got, table, 0, 1)
    return result.reshape(pair_count, rows_y, rows_z, length), energy_total


def shards(i_coeff, j_coeff, pair_orbital, pair_occ):
    fields = jnp.concatenate((i_coeff, j_coeff), 0)
    padded = extended(fields, (("gy", 1), ("gz", 2)), 8)
    own_count = i_coeff.shape[0]
    local_partners = synthesize(padded[own_count:])
    local_count = local_partners.shape[0]
    band_count = lax.axis_size("band")
    mine = lax.axis_index("band") == jnp.arange(band_count, dtype=jnp.int32)[:, None]
    wanted = group_sum(jnp.where(mine, pair_orbital, 0), ("band",))
    first_owned = lax.axis_index("band") * local_count
    slots = jnp.zeros(wanted.shape + local_partners.shape[1:], jnp.float32)
    for number in range(local_count):
        hit = (wanted == first_owned + number)[:, :, None, None, None]
        slots = jnp.where(hit, local_partners[number][None, None], slots)
    arrived = lax.all_to_all(slots, "band", 0, 0, tiled=True)
    owners = wanted[lax.axis_index("band")] // local_count
    partner = jnp.stack(
        [lax.dynamic_index_in_dim(arrived[:, pair], owners[pair], 0, False) for pair in range(owners.shape[0])]
    )
    own_orbital = synthesize(padded[:own_count])[0]
    density = own_orbital[None] * partner
    potential, energy_part = potentials(density)
    weights = pair_occ[0].astype(jnp.float32)
    applied = -jnp.sum(weights[:, None, None, None] * potential * partner, axis=0)
    length = own_orbital.shape[2]
    energy = energy_part / float(length**3)
    return (applied[None], energy[None])


def solution(mesh):
    in_specs = (
        P("band", "gy", "gz", None),
        P("band", "gy", "gz", None),
        P("band", None),
        P("band", None),
    )
    out_specs = (P("band", "gy", "gz", None), P("band", None))
    return jax.shard_map(shards, mesh=mesh, in_specs=in_specs, out_specs=out_specs, check_vma=False)
```

```python
import math

import jax
import jax.numpy as jnp
import numpy as np
from jax import lax
from jax.sharding import PartitionSpec as P

tap_offsets = np.arange(-8, 8)
raw_taps = 0.6 ** np.abs(tap_offsets + 0.5) * np.where(tap_offsets % 2 == 0, 1.0, -0.6)
FILTER_TAPS = raw_taps / np.sqrt(np.sum(raw_taps**2))
SCREEN = 0.001
precise_mode = lax.Precision.HIGHEST
fast_mode = lax.Precision.HIGH


def extended(cells, sides, width):
    for axis, dim in sides:
        count = lax.axis_size(axis)
        extent = cells.shape[dim]
        head = lax.slice_in_dim(cells, 0, width, axis=dim)
        tail = lax.slice_in_dim(cells, extent - width, extent, axis=dim)
        if count == 2:
            first = lax.axis_index(axis) == 0
            got = lax.ppermute(jnp.where(first, tail, head), axis, [(0, 1), (1, 0)])
            empty = jnp.zeros_like(got)
            before = jnp.where(first, empty, got)
            after = jnp.where(first, got, empty)
        else:
            before = lax.ppermute(tail, axis, [(i, i + 1) for i in range(count - 1)])
            after = lax.ppermute(head, axis, [(i + 1, i) for i in range(count - 1)])
        cells = jnp.concatenate([before, cells, after], axis=dim)
    return cells


def group_sum(values, axes):
    total = values
    for axis in axes:
        count = lax.axis_size(axis)
        if count & (count - 1):
            total = lax.psum(total, axis)
            continue
        step = 1
        while step < count:
            total = total + lax.ppermute(total, axis, [(i, i ^ step) for i in range(count)])
            step *= 2
    return total


def band_matrix(row_count, col_count, shift_by):
    row_index = jnp.arange(row_count, dtype=jnp.int32)[:, None]
    col_index = jnp.arange(col_count, dtype=jnp.int32)[None, :]
    offset = row_index - shift_by - col_index
    picked = jnp.zeros((row_count, col_count), jnp.float32)
    for number in range(16):
        picked = picked + jnp.where(offset == number - 8, float(FILTER_TAPS[number]), 0.0)
    return picked


def synthesize(padded):
    wide_y, wide_z, length = (padded.shape[1], padded.shape[2], padded.shape[3])
    matrix_y = band_matrix(wide_y, wide_y - 16, 8)
    matrix_z = band_matrix(wide_z, wide_z - 16, 8)
    matrix_x = band_matrix(length, length, 0)
    step_one = jnp.matmul(padded, matrix_x, precision=precise_mode)
    step_two = jnp.einsum("oyqx,qz->oyzx", step_one, matrix_z, precision=precise_mode)
    return jnp.einsum("oqzx,qy->oyzx", step_two, matrix_y, precision=precise_mode)


def channel_of(channel, length):
    period = 2 * length
    frequency = jnp.where(channel <= length, channel, channel - length)
    angles = 2.0 * math.pi / period * (frequency % period).astype(jnp.float32)
    lattice = 2.0 - 2.0 * jnp.cos(angles)
    fold = jnp.where((channel == 0) | (channel == length), 1.0, 2.0)
    return frequency, lattice, fold


def channel_table(length):
    period = 2 * length
    channel = jnp.arange(period, dtype=jnp.int32)[None, :]
    frequency, _, _ = channel_of(channel, length)
    positions = jnp.arange(length, dtype=jnp.int32)[:, None] * frequency
    angles = 2.0 * math.pi / period * (positions % period).astype(jnp.float32)
    return jnp.where(channel <= length, jnp.cos(angles), jnp.sin(angles))


def contract(left, right, left_dim, right_dim):
    return lax.dot_general(
        left, right, (((left_dim,), (right_dim,)), ((), ())), precision=fast_mode
    )


def potentials(density):
    pair_count, rows_y, rows_z, length = density.shape
    period = 2 * length
    count_y = lax.axis_size("gy")
    count_z = lax.axis_size("gz")
    spread = count_y * count_z
    width = period // spread
    table = channel_table(length)
    flat = density.transpose(0, 2, 1, 3).reshape(pair_count * rows_y * rows_z, length)
    along_x = contract(table, flat, 0, 1)
    send = along_x.reshape(spread, width, pair_count, rows_y * rows_z)
    got = lax.all_to_all(send, ("gy", "gz"), 0, 0, tiled=True)
    got = got.reshape(count_y, count_z, width, pair_count, rows_z, rows_y)
    got = got.transpose(2, 3, 1, 4, 0, 5).reshape(
        width, pair_count, count_z * rows_z, count_y * rows_y
    )
    along_z = contract(got, table, 3, 0)
    spectrum = contract(along_z, table, 2, 0)
    own = lax.axis_index(("gy", "gz")) * width + jnp.arange(width, dtype=jnp.int32)
    _, lattice_x, fold_x = channel_of(own, length)
    _, lattice_all, fold_all = channel_of(jnp.arange(period, dtype=jnp.int32), length)
    weight = (
        fold_x[:, None, None] * fold_all[None, :, None] * fold_all[None, None, :]
    ) / (
        (lattice_x[:, None, None] + lattice_all[None, :, None] + lattice_all[None, None, :] + SCREEN)
        * float(period**3)
    )
    weighted = spectrum * weight[:, None]
    energy_part = jnp.sum(weighted * spectrum, axis=(0, 2, 3))
    back_y = contract(weighted, table, 3, 1)
    back_z = contract(back_y, table, 2, 1)
    back = back_z.reshape(width, pair_count, count_z, rows_z, count_y, rows_y)
    back = back.transpose(4, 2, 0, 1, 5, 3).reshape(spread, width, pair_count, rows_y * rows_z)
    rider = jnp.broadcast_to(energy_part[None, None, :, None], (spread, width, pair_count, 128))
    back = jnp.concatenate((back, rider), axis=3)
    got = lax.all_to_all(back, ("gy", "gz"), 0, 0, tiled=True)
    energy_total = jnp.sum(got[:, 0, :, rows_y * rows_z], axis=0)
    got = got[:, :, :, : rows_y * rows_z].reshape(period, pair_count, rows_y * rows_z)
    result = contract(got, table, 0, 1)
    return result.reshape(pair_count, rows_y, rows_z, length), energy_total


def shards(i_coeff, j_coeff, pair_orbital, pair_occ):
    fields = jnp.concatenate((i_coeff, j_coeff), 0)
    padded = extended(fields, (("gy", 1), ("gz", 2)), 8)
    own_count = i_coeff.shape[0]
    local_partners = synthesize(padded[own_count:])
    local_count = local_partners.shape[0]
    band_count = lax.axis_size("band")
    mine = lax.axis_index("band") == jnp.arange(band_count, dtype=jnp.int32)[:, None]
    wanted = group_sum(jnp.where(mine, pair_orbital, 0), ("band",))
    first_owned = lax.axis_index("band") * local_count
    slots = jnp.zeros(wanted.shape + local_partners.shape[1:], jnp.float32)
    for number in range(local_count):
        hit = (wanted == first_owned + number)[:, :, None, None, None]
        slots = jnp.where(hit, local_partners[number][None, None], slots)
    partner = jnp.sum(lax.all_to_all(slots, "band", 0, 0, tiled=True), axis=0)
    own_orbital = synthesize(padded[:own_count])[0]
    density = own_orbital[None] * partner
    potential, energy_part = potentials(density)
    weights = pair_occ[0].astype(jnp.float32)
    applied = -jnp.sum(weights[:, None, None, None] * potential * partner, axis=0)
    length = own_orbital.shape[2]
    energy = energy_part / float(length**3)
    return (applied[None], energy[None])


def solution(mesh):
    in_specs = (
        P("band", "gy", "gz", None),
        P("band", "gy", "gz", None),
        P("band", None),
        P("band", None),
    )
    out_specs = (P("band", "gy", "gz", None), P("band", None))
    return jax.shard_map(shards, mesh=mesh, in_specs=in_specs, out_specs=out_specs, check_vma=False)
```

```python
import math

import jax
import jax.numpy as jnp
import numpy as np
from jax import lax
from jax.sharding import PartitionSpec as P

tap_offsets = np.arange(-8, 8)
raw_taps = 0.6 ** np.abs(tap_offsets + 0.5) * np.where(tap_offsets % 2 == 0, 1.0, -0.6)
FILTER_TAPS = raw_taps / np.sqrt(np.sum(raw_taps**2))
SCREEN = 0.001
precise_mode = lax.Precision.HIGHEST
fast_mode = lax.Precision.HIGH


def extended(cells, sides, width):
    for axis, dim in sides:
        count = lax.axis_size(axis)
        extent = cells.shape[dim]
        head = lax.slice_in_dim(cells, 0, width, axis=dim)
        tail = lax.slice_in_dim(cells, extent - width, extent, axis=dim)
        if count == 2:
            first = lax.axis_index(axis) == 0
            got = lax.ppermute(jnp.where(first, tail, head), axis, [(0, 1), (1, 0)])
            empty = jnp.zeros_like(got)
            before = jnp.where(first, empty, got)
            after = jnp.where(first, got, empty)
        else:
            before = lax.ppermute(tail, axis, [(i, i + 1) for i in range(count - 1)])
            after = lax.ppermute(head, axis, [(i + 1, i) for i in range(count - 1)])
        cells = jnp.concatenate([before, cells, after], axis=dim)
    return cells


def group_sum(values, axes):
    total = values
    for axis in axes:
        count = lax.axis_size(axis)
        if count & (count - 1):
            total = lax.psum(total, axis)
            continue
        step = 1
        while step < count:
            total = total + lax.ppermute(total, axis, [(i, i ^ step) for i in range(count)])
            step *= 2
    return total


def band_matrix(row_count, col_count, shift_by):
    row_index = jnp.arange(row_count, dtype=jnp.int32)[:, None]
    col_index = jnp.arange(col_count, dtype=jnp.int32)[None, :]
    offset = row_index - shift_by - col_index
    picked = jnp.zeros((row_count, col_count), jnp.float32)
    for number in range(16):
        picked = picked + jnp.where(offset == number - 8, float(FILTER_TAPS[number]), 0.0)
    return picked


def synthesize(padded):
    wide_y, wide_z, length = (padded.shape[1], padded.shape[2], padded.shape[3])
    matrix_y = band_matrix(wide_y, wide_y - 16, 8)
    matrix_z = band_matrix(wide_z, wide_z - 16, 8)
    matrix_x = band_matrix(length, length, 0)
    step_one = jnp.matmul(padded, matrix_x, precision=precise_mode)
    step_two = jnp.einsum("oyqx,qz->oyzx", step_one, matrix_z, precision=precise_mode)
    return jnp.einsum("oqzx,qy->oyzx", step_two, matrix_y, precision=precise_mode)


def channel_of(channel, length):
    period = 2 * length
    frequency = jnp.where(channel <= length, channel, channel - length)
    angles = 2.0 * math.pi / period * (frequency % period).astype(jnp.float32)
    lattice = 2.0 - 2.0 * jnp.cos(angles)
    fold = jnp.where((channel == 0) | (channel == length), 1.0, 2.0)
    return frequency, lattice, fold


def channel_table(length):
    period = 2 * length
    channel = jnp.arange(period, dtype=jnp.int32)[None, :]
    frequency, _, _ = channel_of(channel, length)
    positions = jnp.arange(length, dtype=jnp.int32)[:, None] * frequency
    angles = 2.0 * math.pi / period * (positions % period).astype(jnp.float32)
    return jnp.where(channel <= length, jnp.cos(angles), jnp.sin(angles))


def contract(left, right, left_dim, right_dim):
    return lax.dot_general(
        left, right, (((left_dim,), (right_dim,)), ((), ())), precision=fast_mode
    )


def potentials(density):
    pair_count, rows_y, rows_z, length = density.shape
    period = 2 * length
    count_y = lax.axis_size("gy")
    count_z = lax.axis_size("gz")
    spread = count_y * count_z
    width = period // spread
    table = channel_table(length)
    flat = density.transpose(0, 2, 1, 3).reshape(pair_count * rows_y * rows_z, length)
    along_x = contract(table, flat, 0, 1)
    send = along_x.reshape(spread, width, pair_count, rows_y * rows_z)
    got = lax.all_to_all(send, ("gy", "gz"), 0, 0, tiled=True)
    got = got.reshape(count_y, count_z, width, pair_count, rows_z, rows_y)
    got = got.transpose(2, 3, 1, 4, 0, 5).reshape(
        width, pair_count, count_z * rows_z, count_y * rows_y
    )
    along_z = contract(got, table, 3, 0)
    spectrum = contract(along_z, table, 2, 0)
    own = lax.axis_index(("gy", "gz")) * width + jnp.arange(width, dtype=jnp.int32)
    _, lattice_x, fold_x = channel_of(own, length)
    _, lattice_all, fold_all = channel_of(jnp.arange(period, dtype=jnp.int32), length)
    weight = (
        fold_x[:, None, None] * fold_all[None, :, None] * fold_all[None, None, :]
    ) / (
        (lattice_x[:, None, None] + lattice_all[None, :, None] + lattice_all[None, None, :] + SCREEN)
        * float(period**3)
    )
    weighted = spectrum * weight[:, None]
    energy_part = jnp.sum(weighted * spectrum, axis=(0, 2, 3))
    back_y = contract(weighted, table, 3, 1)
    back_z = contract(back_y, table, 2, 1)
    back = back_z.reshape(width, pair_count, count_z, rows_z, count_y, rows_y)
    back = back.transpose(4, 2, 0, 1, 3, 5).reshape(spread, width, pair_count, rows_y * rows_z)
    rider = jnp.broadcast_to(energy_part[None, None, :, None], (spread, width, pair_count, 128))
    back = jnp.concatenate((back, rider), axis=3)
    got = lax.all_to_all(back, ("gy", "gz"), 0, 0, tiled=True)
    energy_total = jnp.sum(got[:, 0, :, rows_y * rows_z], axis=0)
    got = got[:, :, :, : rows_y * rows_z].reshape(period, pair_count, rows_y * rows_z)
    result = contract(got, table, 0, 1)
    result = result.reshape(pair_count, rows_z, rows_y, length).transpose(0, 2, 1, 3)
    return result, energy_total


def shards(i_coeff, j_coeff, pair_orbital, pair_occ):
    fields = jnp.concatenate((i_coeff, j_coeff), 0)
    padded = extended(fields, (("gy", 1), ("gz", 2)), 8)
    own_count = i_coeff.shape[0]
    local_partners = synthesize(padded[own_count:])
    local_count = local_partners.shape[0]
    band_count = lax.axis_size("band")
    mine = lax.axis_index("band") == jnp.arange(band_count, dtype=jnp.int32)[:, None]
    wanted = group_sum(jnp.where(mine, pair_orbital, 0), ("band",))
    first_owned = lax.axis_index("band") * local_count
    slots = jnp.zeros(wanted.shape + local_partners.shape[1:], jnp.float32)
    for number in range(local_count):
        hit = (wanted == first_owned + number)[:, :, None, None, None]
        slots = jnp.where(hit, local_partners[number][None, None], slots)
    partner = jnp.sum(lax.all_to_all(slots, "band", 0, 0, tiled=True), axis=0)
    own_orbital = synthesize(padded[:own_count])[0]
    density = own_orbital[None] * partner
    potential, energy_part = potentials(density)
    weights = pair_occ[0].astype(jnp.float32)
    applied = -jnp.sum(weights[:, None, None, None] * potential * partner, axis=0)
    length = own_orbital.shape[2]
    energy = energy_part / float(length**3)
    return (applied[None], energy[None])


def solution(mesh):
    in_specs = (
        P("band", "gy", "gz", None),
        P("band", "gy", "gz", None),
        P("band", None),
        P("band", None),
    )
    out_specs = (P("band", "gy", "gz", None), P("band", None))
    return jax.shard_map(shards, mesh=mesh, in_specs=in_specs, out_specs=out_specs, check_vma=False)
```

```python
import math

import jax
import jax.numpy as jnp
import numpy as np
from jax import lax
from jax.sharding import PartitionSpec as P

tap_offsets = np.arange(-8, 8)
raw_taps = 0.6 ** np.abs(tap_offsets + 0.5) * np.where(tap_offsets % 2 == 0, 1.0, -0.6)
FILTER_TAPS = raw_taps / np.sqrt(np.sum(raw_taps**2))
SCREEN = 0.001
precise_mode = lax.Precision.HIGHEST
fast_mode = lax.Precision.HIGH


def extended(cells, sides, width):
    for axis, dim in sides:
        count = lax.axis_size(axis)
        extent = cells.shape[dim]
        head = lax.slice_in_dim(cells, 0, width, axis=dim)
        tail = lax.slice_in_dim(cells, extent - width, extent, axis=dim)
        if count == 2:
            first = lax.axis_index(axis) == 0
            got = lax.ppermute(jnp.where(first, tail, head), axis, [(0, 1), (1, 0)])
            empty = jnp.zeros_like(got)
            before = jnp.where(first, empty, got)
            after = jnp.where(first, got, empty)
        else:
            before = lax.ppermute(tail, axis, [(i, i + 1) for i in range(count - 1)])
            after = lax.ppermute(head, axis, [(i + 1, i) for i in range(count - 1)])
        cells = jnp.concatenate([before, cells, after], axis=dim)
    return cells


def group_sum(values, axes):
    total = values
    for axis in axes:
        count = lax.axis_size(axis)
        if count & (count - 1):
            total = lax.psum(total, axis)
            continue
        step = 1
        while step < count:
            total = total + lax.ppermute(total, axis, [(i, i ^ step) for i in range(count)])
            step *= 2
    return total


def band_matrix(row_count, col_count, shift_by):
    row_index = jnp.arange(row_count, dtype=jnp.int32)[:, None]
    col_index = jnp.arange(col_count, dtype=jnp.int32)[None, :]
    offset = row_index - shift_by - col_index
    picked = jnp.zeros((row_count, col_count), jnp.float32)
    for number in range(16):
        picked = picked + jnp.where(offset == number - 8, float(FILTER_TAPS[number]), 0.0)
    return picked


def synthesize(padded):
    wide_y, wide_z, length = (padded.shape[1], padded.shape[2], padded.shape[3])
    matrix_y = band_matrix(wide_y, wide_y - 16, 8)
    matrix_z = band_matrix(wide_z, wide_z - 16, 8)
    matrix_x = band_matrix(length, length, 0)
    step_one = jnp.matmul(padded, matrix_x, precision=precise_mode)
    step_two = jnp.einsum("oyqx,qz->oyzx", step_one, matrix_z, precision=precise_mode)
    return jnp.einsum("oqzx,qy->oyzx", step_two, matrix_y, precision=precise_mode)


def channel_of(channel, length):
    period = 2 * length
    frequency = jnp.where(channel <= length, channel, channel - length)
    angles = 2.0 * math.pi / period * (frequency % period).astype(jnp.float32)
    lattice = 2.0 - 2.0 * jnp.cos(angles)
    fold = jnp.where((channel == 0) | (channel == length), 1.0, 2.0)
    return frequency, lattice, fold


def channel_table(length):
    period = 2 * length
    channel = jnp.arange(period, dtype=jnp.int32)[None, :]
    frequency, _, _ = channel_of(channel, length)
    positions = jnp.arange(length, dtype=jnp.int32)[:, None] * frequency
    angles = 2.0 * math.pi / period * (positions % period).astype(jnp.float32)
    return jnp.where(channel <= length, jnp.cos(angles), jnp.sin(angles))


def contract(left, right, left_dim, right_dim):
    return lax.dot_general(
        left, right, (((left_dim,), (right_dim,)), ((), ())), precision=fast_mode
    )


def potentials(density):
    pair_count, rows_y, rows_z, length = density.shape
    period = 2 * length
    count_y = lax.axis_size("gy")
    count_z = lax.axis_size("gz")
    spread = count_y * count_z
    width = period // spread
    table = channel_table(length)
    flat = density.transpose(0, 2, 1, 3).reshape(pair_count * rows_y * rows_z, length)
    along_x = contract(table, flat, 0, 1)
    send = along_x.reshape(spread, width, pair_count, rows_y * rows_z)
    got = lax.all_to_all(send, ("gy", "gz"), 0, 0, tiled=True)
    got = got.reshape(count_y, count_z, width, pair_count, rows_z, rows_y)
    got = got.transpose(2, 3, 1, 4, 0, 5).reshape(
        width, pair_count, count_z * rows_z, count_y * rows_y
    )
    along_z = contract(got, table, 3, 0)
    spectrum = contract(along_z, table, 2, 0)
    own = lax.axis_index(("gy", "gz")) * width + jnp.arange(width, dtype=jnp.int32)
    _, lattice_x, fold_x = channel_of(own, length)
    _, lattice_all, fold_all = channel_of(jnp.arange(period, dtype=jnp.int32), length)
    weight = (
        fold_x[:, None, None] * fold_all[None, :, None] * fold_all[None, None, :]
    ) / (
        (lattice_x[:, None, None] + lattice_all[None, :, None] + lattice_all[None, None, :] + SCREEN)
        * float(period**3)
    )
    weighted = spectrum * weight[:, None]
    energy_part = jnp.sum(weighted * spectrum, axis=(0, 2, 3))
    back_y = contract(weighted, table, 3, 1)
    back_z = contract(back_y, table, 2, 1)
    back = back_z.reshape(width, pair_count, count_z, rows_z, count_y, rows_y)
    back = back.transpose(4, 2, 0, 1, 3, 5).reshape(spread, width, pair_count, rows_y * rows_z)
    rider = jnp.broadcast_to(energy_part[None, None, :, None], (spread, width, pair_count, 128))
    back = jnp.concatenate((back, rider), axis=3)
    got = lax.all_to_all(back, ("gy", "gz"), 0, 0, tiled=True)
    energy_total = jnp.sum(got[:, 0, :, rows_y * rows_z], axis=0)
    got = got[:, :, :, : rows_y * rows_z].reshape(period, pair_count, rows_y * rows_z)
    result = contract(got, table, 0, 1)
    result = result.reshape(pair_count, rows_z, rows_y, length).transpose(0, 2, 1, 3)
    return result, energy_total


def shards(i_coeff, j_coeff, pair_orbital, pair_occ):
    sides = (("gy", 1), ("gz", 2))
    local_count = j_coeff.shape[0]
    band_count = lax.axis_size("band")
    mine = lax.axis_index("band") == jnp.arange(band_count, dtype=jnp.int32)[:, None]
    wanted = group_sum(jnp.where(mine, pair_orbital, 0), ("band",))
    first_owned = lax.axis_index("band") * local_count
    slots = jnp.zeros(wanted.shape + j_coeff.shape[1:], jnp.float32)
    for number in range(local_count):
        hit = (wanted == first_owned + number)[:, :, None, None, None]
        slots = jnp.where(hit, j_coeff[number][None, None], slots)
    arrived = lax.all_to_all(slots, "band", 0, 0, tiled=True)
    own_orbital = synthesize(extended(i_coeff, sides, 8))[0]
    partner = synthesize(extended(jnp.sum(arrived, axis=0), sides, 8))
    density = own_orbital[None] * partner
    potential, energy_part = potentials(density)
    weights = pair_occ[0].astype(jnp.float32)
    applied = -jnp.sum(weights[:, None, None, None] * potential * partner, axis=0)
    length = own_orbital.shape[2]
    energy = energy_part / float(length**3)
    return (applied[None], energy[None])


def solution(mesh):
    in_specs = (
        P("band", "gy", "gz", None),
        P("band", "gy", "gz", None),
        P("band", None),
        P("band", None),
    )
    out_specs = (P("band", "gy", "gz", None), P("band", None))
    return jax.shard_map(shards, mesh=mesh, in_specs=in_specs, out_specs=out_specs, check_vma=False)
```

```python
import math

import jax
import jax.numpy as jnp
import numpy as np
from jax import lax
from jax.sharding import PartitionSpec as P

tap_offsets = np.arange(-8, 8)
raw_taps = 0.6 ** np.abs(tap_offsets + 0.5) * np.where(tap_offsets % 2 == 0, 1.0, -0.6)
FILTER_TAPS = raw_taps / np.sqrt(np.sum(raw_taps**2))
SCREEN = 0.001
precise_mode = lax.Precision.HIGHEST
fast_mode = lax.Precision.HIGH


def extended(cells, sides, width):
    for axis, dim in sides:
        count = lax.axis_size(axis)
        extent = cells.shape[dim]
        head = lax.slice_in_dim(cells, 0, width, axis=dim)
        tail = lax.slice_in_dim(cells, extent - width, extent, axis=dim)
        if count == 2:
            first = lax.axis_index(axis) == 0
            got = lax.ppermute(jnp.where(first, tail, head), axis, [(0, 1), (1, 0)])
            empty = jnp.zeros_like(got)
            before = jnp.where(first, empty, got)
            after = jnp.where(first, got, empty)
        else:
            before = lax.ppermute(tail, axis, [(i, i + 1) for i in range(count - 1)])
            after = lax.ppermute(head, axis, [(i + 1, i) for i in range(count - 1)])
        cells = jnp.concatenate([before, cells, after], axis=dim)
    return cells


def group_sum(values, axes):
    total = values
    for axis in axes:
        count = lax.axis_size(axis)
        if count & (count - 1):
            total = lax.psum(total, axis)
            continue
        step = 1
        while step < count:
            total = total + lax.ppermute(total, axis, [(i, i ^ step) for i in range(count)])
            step *= 2
    return total


def band_matrix(row_count, col_count, shift_by):
    row_index = jnp.arange(row_count, dtype=jnp.int32)[:, None]
    col_index = jnp.arange(col_count, dtype=jnp.int32)[None, :]
    offset = row_index - shift_by - col_index
    picked = jnp.zeros((row_count, col_count), jnp.float32)
    for number in range(16):
        picked = picked + jnp.where(offset == number - 8, float(FILTER_TAPS[number]), 0.0)
    return picked


def synthesize(padded):
    wide_y, wide_z, length = (padded.shape[1], padded.shape[2], padded.shape[3])
    matrix_y = band_matrix(wide_y, wide_y - 16, 8)
    matrix_z = band_matrix(wide_z, wide_z - 16, 8)
    matrix_x = band_matrix(length, length, 0)
    step_one = jnp.matmul(padded, matrix_x, precision=precise_mode)
    step_two = jnp.einsum("oyqx,qz->oyzx", step_one, matrix_z, precision=precise_mode)
    return jnp.einsum("oqzx,qy->oyzx", step_two, matrix_y, precision=precise_mode)


def channel_of(channel, length):
    period = 2 * length
    frequency = jnp.where(channel <= length, channel, channel - length)
    angles = 2.0 * math.pi / period * (frequency % period).astype(jnp.float32)
    lattice = 2.0 - 2.0 * jnp.cos(angles)
    fold = jnp.where((channel == 0) | (channel == length), 1.0, 2.0)
    return frequency, lattice, fold


def channel_table(length):
    period = 2 * length
    channel = jnp.arange(period, dtype=jnp.int32)[None, :]
    frequency, _, _ = channel_of(channel, length)
    positions = jnp.arange(length, dtype=jnp.int32)[:, None] * frequency
    angles = 2.0 * math.pi / period * (positions % period).astype(jnp.float32)
    return jnp.where(channel <= length, jnp.cos(angles), jnp.sin(angles))


def contract(left, right, left_dim, right_dim):
    return lax.dot_general(
        left, right, (((left_dim,), (right_dim,)), ((), ())), precision=fast_mode
    )


def potentials(density):
    pair_count, rows_y, rows_z, length = density.shape
    period = 2 * length
    count_y = lax.axis_size("gy")
    count_z = lax.axis_size("gz")
    spread = count_y * count_z
    width = period // spread
    table = channel_table(length)
    flat = density.transpose(0, 2, 1, 3).reshape(pair_count * rows_y * rows_z, length)
    along_x = contract(table, flat, 0, 1)
    send = along_x.reshape(spread, width, pair_count, rows_y * rows_z)
    got = lax.all_to_all(send, ("gy", "gz"), 0, 0, tiled=True)
    got = got.reshape(count_y, count_z, width, pair_count, rows_z, rows_y)
    got = got.transpose(2, 3, 1, 4, 0, 5).reshape(
        width, pair_count, count_z * rows_z, count_y * rows_y
    )
    along_z = contract(got, table, 3, 0)
    spectrum = contract(along_z, table, 2, 0)
    own = lax.axis_index(("gy", "gz")) * width + jnp.arange(width, dtype=jnp.int32)
    _, lattice_x, fold_x = channel_of(own, length)
    _, lattice_all, fold_all = channel_of(jnp.arange(period, dtype=jnp.int32), length)
    weight = (
        fold_x[:, None, None] * fold_all[None, :, None] * fold_all[None, None, :]
    ) / (
        (lattice_x[:, None, None] + lattice_all[None, :, None] + lattice_all[None, None, :] + SCREEN)
        * float(period**3)
    )
    weighted = spectrum * weight[:, None]
    energy_part = jnp.sum(weighted * spectrum, axis=(0, 2, 3))
    back_y = contract(weighted, table, 3, 1)
    back_z = contract(back_y, table, 2, 1)
    back = back_z.reshape(width, pair_count, count_z, rows_z, count_y, rows_y)
    back = back.transpose(4, 2, 0, 1, 3, 5).reshape(spread, width, pair_count, rows_y * rows_z)
    rider = jnp.broadcast_to(energy_part[None, None, :, None], (spread, width, pair_count, 128))
    back = jnp.concatenate((back, rider), axis=3)
    got = lax.all_to_all(back, ("gy", "gz"), 0, 0, tiled=True)
    energy_total = jnp.sum(got[:, 0, :, rows_y * rows_z], axis=0)
    got = got[:, :, :, : rows_y * rows_z].reshape(period, pair_count, rows_y * rows_z)
    result = contract(got, table, 0, 1)
    result = result.reshape(pair_count, rows_z, rows_y, length).transpose(0, 2, 1, 3)
    return result, energy_total


def shards(i_coeff, j_coeff, pair_orbital, pair_occ):
    sides = (("gy", 1), ("gz", 2))
    local_count = j_coeff.shape[0]
    band_count = lax.axis_size("band")
    requests = jnp.broadcast_to(pair_orbital, (band_count,) + pair_orbital.shape[1:])
    wanted = lax.all_to_all(requests, "band", 0, 0, tiled=True)
    first_owned = lax.axis_index("band") * local_count
    slots = jnp.zeros(wanted.shape + j_coeff.shape[1:], jnp.float32)
    for number in range(local_count):
        hit = (wanted == first_owned + number)[:, :, None, None, None]
        slots = jnp.where(hit, j_coeff[number][None, None], slots)
    arrived = lax.all_to_all(slots, "band", 0, 0, tiled=True)
    own_orbital = synthesize(extended(i_coeff, sides, 8))[0]
    partner = synthesize(extended(jnp.sum(arrived, axis=0), sides, 8))
    density = own_orbital[None] * partner
    potential, energy_part = potentials(density)
    weights = pair_occ[0].astype(jnp.float32)
    applied = -jnp.sum(weights[:, None, None, None] * potential * partner, axis=0)
    length = own_orbital.shape[2]
    energy = energy_part / float(length**3)
    return (applied[None], energy[None])


def solution(mesh):
    in_specs = (
        P("band", "gy", "gz", None),
        P("band", "gy", "gz", None),
        P("band", None),
        P("band", None),
    )
    out_specs = (P("band", "gy", "gz", None), P("band", None))
    return jax.shard_map(shards, mesh=mesh, in_specs=in_specs, out_specs=out_specs, check_vma=False)
```

```python
import math

import jax
import jax.numpy as jnp
import numpy as np
from jax import lax
from jax.sharding import PartitionSpec as P

tap_offsets = np.arange(-8, 8)
raw_taps = 0.6 ** np.abs(tap_offsets + 0.5) * np.where(tap_offsets % 2 == 0, 1.0, -0.6)
FILTER_TAPS = raw_taps / np.sqrt(np.sum(raw_taps**2))
SCREEN = 0.001
precise_mode = lax.Precision.HIGHEST
fast_mode = lax.Precision.HIGH


def extended(cells, sides, width):
    for axis, dim in sides:
        count = lax.axis_size(axis)
        extent = cells.shape[dim]
        head = lax.slice_in_dim(cells, 0, width, axis=dim)
        tail = lax.slice_in_dim(cells, extent - width, extent, axis=dim)
        if count == 2:
            first = lax.axis_index(axis) == 0
            got = lax.ppermute(jnp.where(first, tail, head), axis, [(0, 1), (1, 0)])
            empty = jnp.zeros_like(got)
            before = jnp.where(first, empty, got)
            after = jnp.where(first, got, empty)
        else:
            before = lax.ppermute(tail, axis, [(i, i + 1) for i in range(count - 1)])
            after = lax.ppermute(head, axis, [(i + 1, i) for i in range(count - 1)])
        cells = jnp.concatenate([before, cells, after], axis=dim)
    return cells


def group_sum(values, axes):
    total = values
    for axis in axes:
        count = lax.axis_size(axis)
        if count & (count - 1):
            total = lax.psum(total, axis)
            continue
        step = 1
        while step < count:
            total = total + lax.ppermute(total, axis, [(i, i ^ step) for i in range(count)])
            step *= 2
    return total


def band_matrix(row_count, col_count, shift_by):
    row_index = jnp.arange(row_count, dtype=jnp.int32)[:, None]
    col_index = jnp.arange(col_count, dtype=jnp.int32)[None, :]
    offset = row_index - shift_by - col_index
    picked = jnp.zeros((row_count, col_count), jnp.float32)
    for number in range(16):
        picked = picked + jnp.where(offset == number - 8, float(FILTER_TAPS[number]), 0.0)
    return picked


def filter_x(cells):
    length = cells.shape[3]
    return jnp.matmul(cells, band_matrix(length, length, 0), precision=precise_mode)


def filter_yz(padded):
    wide_y, wide_z = padded.shape[1], padded.shape[2]
    matrix_y = band_matrix(wide_y, wide_y - 16, 8)
    matrix_z = band_matrix(wide_z, wide_z - 16, 8)
    step_one = jnp.einsum("oyqx,qz->oyzx", padded, matrix_z, precision=precise_mode)
    return jnp.einsum("oqzx,qy->oyzx", step_one, matrix_y, precision=precise_mode)


def channel_of(channel, length):
    period = 2 * length
    frequency = jnp.where(channel <= length, channel, channel - length)
    angles = 2.0 * math.pi / period * (frequency % period).astype(jnp.float32)
    lattice = 2.0 - 2.0 * jnp.cos(angles)
    fold = jnp.where((channel == 0) | (channel == length), 1.0, 2.0)
    return frequency, lattice, fold


def channel_table(length):
    period = 2 * length
    channel = jnp.arange(period, dtype=jnp.int32)[None, :]
    frequency, _, _ = channel_of(channel, length)
    positions = jnp.arange(length, dtype=jnp.int32)[:, None] * frequency
    angles = 2.0 * math.pi / period * (positions % period).astype(jnp.float32)
    return jnp.where(channel <= length, jnp.cos(angles), jnp.sin(angles))


def contract(left, right, left_dim, right_dim):
    return lax.dot_general(
        left, right, (((left_dim,), (right_dim,)), ((), ())), precision=fast_mode
    )


def potentials(density):
    pair_count, rows_y, rows_z, length = density.shape
    period = 2 * length
    count_y = lax.axis_size("gy")
    count_z = lax.axis_size("gz")
    spread = count_y * count_z
    width = period // spread
    table = channel_table(length)
    flat = density.transpose(0, 2, 1, 3).reshape(pair_count * rows_y * rows_z, length)
    along_x = contract(table, flat, 0, 1)
    send = along_x.reshape(spread, width, pair_count, rows_y * rows_z)
    got = lax.all_to_all(send, ("gy", "gz"), 0, 0, tiled=True)
    got = got.reshape(count_y, count_z, width, pair_count, rows_z, rows_y)
    got = got.transpose(2, 3, 1, 4, 0, 5).reshape(
        width, pair_count, count_z * rows_z, count_y * rows_y
    )
    along_z = contract(got, table, 3, 0)
    spectrum = contract(along_z, table, 2, 0)
    own = lax.axis_index(("gy", "gz")) * width + jnp.arange(width, dtype=jnp.int32)
    _, lattice_x, fold_x = channel_of(own, length)
    _, lattice_all, fold_all = channel_of(jnp.arange(period, dtype=jnp.int32), length)
    weight = (
        fold_x[:, None, None] * fold_all[None, :, None] * fold_all[None, None, :]
    ) / (
        (lattice_x[:, None, None] + lattice_all[None, :, None] + lattice_all[None, None, :] + SCREEN)
        * float(period**3)
    )
    weighted = spectrum * weight[:, None]
    energy_part = jnp.sum(weighted * spectrum, axis=(0, 2, 3))
    back_y = contract(weighted, table, 3, 1)
    back_z = contract(back_y, table, 2, 1)
    back = back_z.reshape(width, pair_count, count_z, rows_z, count_y, rows_y)
    back = back.transpose(4, 2, 0, 1, 3, 5).reshape(spread, width, pair_count, rows_y * rows_z)
    rider = jnp.broadcast_to(energy_part[None, None, :, None], (spread, width, pair_count, 128))
    back = jnp.concatenate((back, rider), axis=3)
    got = lax.all_to_all(back, ("gy", "gz"), 0, 0, tiled=True)
    energy_total = jnp.sum(got[:, 0, :, rows_y * rows_z], axis=0)
    got = got[:, :, :, : rows_y * rows_z].reshape(period, pair_count, rows_y * rows_z)
    result = contract(got, table, 0, 1)
    result = result.reshape(pair_count, rows_z, rows_y, length).transpose(0, 2, 1, 3)
    return result, energy_total


def shards(i_coeff, j_coeff, pair_orbital, pair_occ):
    sides = (("gy", 1), ("gz", 2))
    local_count = j_coeff.shape[0]
    band_count = lax.axis_size("band")
    mine = lax.axis_index("band") == jnp.arange(band_count, dtype=jnp.int32)[:, None]
    wanted = group_sum(jnp.where(mine, pair_orbital, 0), ("band",))
    first_owned = lax.axis_index("band") * local_count
    filtered = filter_x(j_coeff)
    slots = jnp.zeros(wanted.shape + j_coeff.shape[1:], jnp.float32)
    for number in range(local_count):
        hit = (wanted == first_owned + number)[:, :, None, None, None]
        slots = jnp.where(hit, filtered[number][None, None], slots)
    arrived = lax.all_to_all(slots, "band", 0, 0, tiled=True)
    own_orbital = filter_yz(extended(filter_x(i_coeff), sides, 8))[0]
    partner = filter_yz(extended(jnp.sum(arrived, axis=0), sides, 8))
    density = own_orbital[None] * partner
    potential, energy_part = potentials(density)
    weights = pair_occ[0].astype(jnp.float32)
    applied = -jnp.sum(weights[:, None, None, None] * potential * partner, axis=0)
    length = own_orbital.shape[2]
    energy = energy_part / float(length**3)
    return (applied[None], energy[None])


def solution(mesh):
    in_specs = (
        P("band", "gy", "gz", None),
        P("band", "gy", "gz", None),
        P("band", None),
        P("band", None),
    )
    out_specs = (P("band", "gy", "gz", None), P("band", None))
    return jax.shard_map(shards, mesh=mesh, in_specs=in_specs, out_specs=out_specs, check_vma=False)
```

```python
import math

import jax
import jax.numpy as jnp
import numpy as np
from jax import lax
from jax.sharding import PartitionSpec as P

tap_offsets = np.arange(-8, 8)
raw_taps = 0.6 ** np.abs(tap_offsets + 0.5) * np.where(tap_offsets % 2 == 0, 1.0, -0.6)
FILTER_TAPS = raw_taps / np.sqrt(np.sum(raw_taps**2))
SCREEN = 0.001
precise_mode = lax.Precision.HIGHEST
fast_mode = lax.Precision.HIGH


def extended(cells, sides, width):
    for axis, dim in sides:
        count = lax.axis_size(axis)
        extent = cells.shape[dim]
        head = lax.slice_in_dim(cells, 0, width, axis=dim)
        tail = lax.slice_in_dim(cells, extent - width, extent, axis=dim)
        if count == 2:
            first = lax.axis_index(axis) == 0
            got = lax.ppermute(jnp.where(first, tail, head), axis, [(0, 1), (1, 0)])
            empty = jnp.zeros_like(got)
            before = jnp.where(first, empty, got)
            after = jnp.where(first, got, empty)
        else:
            before = lax.ppermute(tail, axis, [(i, i + 1) for i in range(count - 1)])
            after = lax.ppermute(head, axis, [(i + 1, i) for i in range(count - 1)])
        cells = jnp.concatenate([before, cells, after], axis=dim)
    return cells


def group_sum(values, axes):
    total = values
    for axis in axes:
        count = lax.axis_size(axis)
        if count & (count - 1):
            total = lax.psum(total, axis)
            continue
        step = 1
        while step < count:
            total = total + lax.ppermute(total, axis, [(i, i ^ step) for i in range(count)])
            step *= 2
    return total


def band_matrix(row_count, col_count, shift_by):
    row_index = jnp.arange(row_count, dtype=jnp.int32)[:, None]
    col_index = jnp.arange(col_count, dtype=jnp.int32)[None, :]
    offset = row_index - shift_by - col_index
    picked = jnp.zeros((row_count, col_count), jnp.float32)
    for number in range(16):
        picked = picked + jnp.where(offset == number - 8, float(FILTER_TAPS[number]), 0.0)
    return picked


def synthesize(padded):
    wide_y, wide_z, length = (padded.shape[1], padded.shape[2], padded.shape[3])
    matrix_y = band_matrix(wide_y, wide_y - 16, 8)
    matrix_z = band_matrix(wide_z, wide_z - 16, 8)
    matrix_x = band_matrix(length, length, 0)
    step_one = jnp.matmul(padded, matrix_x, precision=precise_mode)
    step_two = jnp.einsum("oyqx,qz->oyzx", step_one, matrix_z, precision=precise_mode)
    return jnp.einsum("oqzx,qy->oyzx", step_two, matrix_y, precision=precise_mode)


def channel_of(channel, length):
    period = 2 * length
    frequency = jnp.where(channel <= length, channel, channel - length)
    angles = 2.0 * math.pi / period * (frequency % period).astype(jnp.float32)
    lattice = 2.0 - 2.0 * jnp.cos(angles)
    fold = jnp.where((channel == 0) | (channel == length), 1.0, 2.0)
    return frequency, lattice, fold


def channel_table(length):
    period = 2 * length
    channel = jnp.arange(period, dtype=jnp.int32)[None, :]
    frequency, _, _ = channel_of(channel, length)
    positions = jnp.arange(length, dtype=jnp.int32)[:, None] * frequency
    angles = 2.0 * math.pi / period * (positions % period).astype(jnp.float32)
    return jnp.where(channel <= length, jnp.cos(angles), jnp.sin(angles))


def contract(left, right, left_dim, right_dim):
    return lax.dot_general(
        left, right, (((left_dim,), (right_dim,)), ((), ())), precision=fast_mode
    )


def potentials(density):
    pair_count, rows_y, rows_z, length = density.shape
    period = 2 * length
    count_y = lax.axis_size("gy")
    count_z = lax.axis_size("gz")
    spread = count_y * count_z
    width = period // spread
    table = channel_table(length)
    flat = density.transpose(0, 2, 1, 3).reshape(pair_count * rows_y * rows_z, length)
    along_x = contract(table, flat, 0, 1)
    send = along_x.reshape(spread, width, pair_count, rows_y * rows_z)
    got = lax.all_to_all(send, ("gy", "gz"), 0, 0, tiled=True)
    got = got.reshape(count_y, count_z, width, pair_count, rows_z, rows_y)
    got = got.transpose(2, 3, 1, 4, 0, 5).reshape(
        width, pair_count, count_z * rows_z, count_y * rows_y
    )
    along_z = contract(got, table, 3, 0)
    spectrum = contract(along_z, table, 2, 0)
    own = lax.axis_index(("gy", "gz")) * width + jnp.arange(width, dtype=jnp.int32)
    _, lattice_x, fold_x = channel_of(own, length)
    _, lattice_all, fold_all = channel_of(jnp.arange(period, dtype=jnp.int32), length)
    weight = (
        fold_x[:, None, None] * fold_all[None, :, None] * fold_all[None, None, :]
    ) / (
        (lattice_x[:, None, None] + lattice_all[None, :, None] + lattice_all[None, None, :] + SCREEN)
        * float(period**3)
    )
    weighted = spectrum * weight[:, None]
    energy_part = jnp.sum(weighted * spectrum, axis=(0, 2, 3))
    back_y = contract(weighted, table, 3, 1)
    back_z = contract(back_y, table, 2, 1)
    back = back_z.reshape(width, pair_count, count_z, rows_z, count_y, rows_y)
    back = back.transpose(4, 2, 0, 1, 3, 5).reshape(spread, width, pair_count, rows_y * rows_z)
    rider = jnp.broadcast_to(energy_part[None, None, :, None], (spread, width, pair_count, 128))
    back = jnp.concatenate((back, rider), axis=3)
    got = lax.all_to_all(back, ("gy", "gz"), 0, 0, tiled=True)
    energy_total = jnp.sum(got[:, 0, :, rows_y * rows_z], axis=0)
    got = got[:, :, :, : rows_y * rows_z].reshape(period, pair_count, rows_y * rows_z)
    result = contract(got, table, 0, 1)
    result = result.reshape(pair_count, rows_z, rows_y, length).transpose(0, 2, 1, 3)
    return result, energy_total


def shards(i_coeff, j_coeff, pair_orbital, pair_occ):
    sides = (("gy", 1), ("gz", 2))
    local_count = j_coeff.shape[0]
    band_count = lax.axis_size("band")
    mine = lax.axis_index("band") == jnp.arange(band_count, dtype=jnp.int32)[:, None]
    wanted = group_sum(jnp.where(mine, pair_orbital, 0), ("band",))
    first_owned = lax.axis_index("band") * local_count
    slots = jnp.zeros(wanted.shape + j_coeff.shape[1:], jnp.float32)
    for number in range(local_count):
        hit = (wanted == first_owned + number)[:, :, None, None, None]
        slots = jnp.where(hit, j_coeff[number][None, None], slots)
    arrived = lax.all_to_all(slots, "band", 0, 0, tiled=True)
    own_orbital = synthesize(extended(i_coeff, sides, 8))[0]
    owners = wanted[lax.axis_index("band")] // local_count
    picked = jnp.stack(
        [lax.dynamic_index_in_dim(arrived[:, pair], owners[pair], 0, False) for pair in range(owners.shape[0])]
    )
    partner = synthesize(extended(picked, sides, 8))
    density = own_orbital[None] * partner
    potential, energy_part = potentials(density)
    weights = pair_occ[0].astype(jnp.float32)
    applied = -jnp.sum(weights[:, None, None, None] * potential * partner, axis=0)
    length = own_orbital.shape[2]
    energy = energy_part / float(length**3)
    return (applied[None], energy[None])


def solution(mesh):
    in_specs = (
        P("band", "gy", "gz", None),
        P("band", "gy", "gz", None),
        P("band", None),
        P("band", None),
    )
    out_specs = (P("band", "gy", "gz", None), P("band", None))
    return jax.shard_map(shards, mesh=mesh, in_specs=in_specs, out_specs=out_specs, check_vma=False)
```

```python
import math

import jax
import jax.numpy as jnp
import numpy as np
from jax import lax
from jax.sharding import PartitionSpec as P

tap_offsets = np.arange(-8, 8)
raw_taps = 0.6 ** np.abs(tap_offsets + 0.5) * np.where(tap_offsets % 2 == 0, 1.0, -0.6)
FILTER_TAPS = raw_taps / np.sqrt(np.sum(raw_taps**2))
SCREEN = 0.001
precise_mode = lax.Precision.HIGHEST
fast_mode = lax.Precision.HIGH


def extended(cells, sides, width):
    for axis, dim in sides:
        count = lax.axis_size(axis)
        extent = cells.shape[dim]
        head = lax.slice_in_dim(cells, 0, width, axis=dim)
        tail = lax.slice_in_dim(cells, extent - width, extent, axis=dim)
        if count == 2:
            first = lax.axis_index(axis) == 0
            got = lax.ppermute(jnp.where(first, tail, head), axis, [(0, 1), (1, 0)])
            empty = jnp.zeros_like(got)
            before = jnp.where(first, empty, got)
            after = jnp.where(first, got, empty)
        else:
            before = lax.ppermute(tail, axis, [(i, i + 1) for i in range(count - 1)])
            after = lax.ppermute(head, axis, [(i + 1, i) for i in range(count - 1)])
        cells = jnp.concatenate([before, cells, after], axis=dim)
    return cells


def group_sum(values, axes):
    total = values
    for axis in axes:
        count = lax.axis_size(axis)
        if count & (count - 1):
            total = lax.psum(total, axis)
            continue
        step = 1
        while step < count:
            total = total + lax.ppermute(total, axis, [(i, i ^ step) for i in range(count)])
            step *= 2
    return total


def band_matrix(row_count, col_count, shift_by):
    row_index = jnp.arange(row_count, dtype=jnp.int32)[:, None]
    col_index = jnp.arange(col_count, dtype=jnp.int32)[None, :]
    offset = row_index - shift_by - col_index
    picked = jnp.zeros((row_count, col_count), jnp.float32)
    for number in range(16):
        picked = picked + jnp.where(offset == number - 8, float(FILTER_TAPS[number]), 0.0)
    return picked


def synthesize(padded):
    wide_y, wide_z, length = (padded.shape[1], padded.shape[2], padded.shape[3])
    matrix_y = band_matrix(wide_y, wide_y - 16, 8)
    matrix_z = band_matrix(wide_z, wide_z - 16, 8)
    matrix_x = band_matrix(length, length, 0)
    step_one = jnp.matmul(padded, matrix_x, precision=precise_mode)
    step_two = jnp.einsum("oyqx,qz->oyzx", step_one, matrix_z, precision=precise_mode)
    return jnp.einsum("oqzx,qy->oyzx", step_two, matrix_y, precision=precise_mode)


def channel_of(channel, length):
    period = 2 * length
    frequency = jnp.where(channel <= length, channel, channel - length)
    angles = 2.0 * math.pi / period * (frequency % period).astype(jnp.float32)
    lattice = 2.0 - 2.0 * jnp.cos(angles)
    fold = jnp.where((channel == 0) | (channel == length), 1.0, 2.0)
    return frequency, lattice, fold


def channel_table(length):
    period = 2 * length
    channel = jnp.arange(period, dtype=jnp.int32)[None, :]
    frequency, _, _ = channel_of(channel, length)
    positions = jnp.arange(length, dtype=jnp.int32)[:, None] * frequency
    angles = 2.0 * math.pi / period * (positions % period).astype(jnp.float32)
    return jnp.where(channel <= length, jnp.cos(angles), jnp.sin(angles))


def contract(left, right, left_dim, right_dim):
    return lax.dot_general(
        left, right, (((left_dim,), (right_dim,)), ((), ())), precision=fast_mode
    )


def potentials(density):
    pair_count, rows_y, rows_z, length = density.shape
    period = 2 * length
    count_y = lax.axis_size("gy")
    count_z = lax.axis_size("gz")
    spread = count_y * count_z
    width = period // spread
    table = channel_table(length)
    flat = density.transpose(0, 2, 1, 3).reshape(pair_count * rows_y * rows_z, length)
    along_x = contract(table, flat, 0, 1)
    send = along_x.reshape(spread, width, pair_count, rows_y * rows_z)
    got = lax.all_to_all(send, ("gy", "gz"), 0, 0, tiled=True)
    got = got.reshape(count_y, count_z, width, pair_count, rows_z, rows_y)
    got = got.transpose(2, 3, 1, 4, 0, 5).reshape(
        width, pair_count, count_z * rows_z, count_y * rows_y
    )
    along_z = contract(got, table, 3, 0)
    spectrum = contract(along_z, table, 2, 0)
    own = lax.axis_index(("gy", "gz")) * width + jnp.arange(width, dtype=jnp.int32)
    _, lattice_x, fold_x = channel_of(own, length)
    _, lattice_all, fold_all = channel_of(jnp.arange(period, dtype=jnp.int32), length)
    weight = (
        fold_x[:, None, None] * fold_all[None, :, None] * fold_all[None, None, :]
    ) / (
        (lattice_x[:, None, None] + lattice_all[None, :, None] + lattice_all[None, None, :] + SCREEN)
        * float(period**3)
    )
    weighted = spectrum * weight[:, None]
    energy_part = jnp.sum(weighted * spectrum, axis=(0, 2, 3))
    back_y = contract(weighted, table, 3, 1)
    back_z = contract(back_y, table, 2, 1)
    back = back_z.reshape(width, pair_count, count_z, rows_z, count_y, rows_y)
    back = back.transpose(4, 2, 0, 1, 3, 5).reshape(spread, width, pair_count, rows_y * rows_z)
    energy_total = group_sum(energy_part, ("gz", "gy"))
    got = lax.all_to_all(back, ("gy", "gz"), 0, 0, tiled=True)
    got = got.reshape(period, pair_count, rows_y * rows_z)
    result = contract(got, table, 0, 1)
    result = result.reshape(pair_count, rows_z, rows_y, length).transpose(0, 2, 1, 3)
    return result, energy_total


def shards(i_coeff, j_coeff, pair_orbital, pair_occ):
    sides = (("gy", 1), ("gz", 2))
    local_count = j_coeff.shape[0]
    band_count = lax.axis_size("band")
    mine = lax.axis_index("band") == jnp.arange(band_count, dtype=jnp.int32)[:, None]
    wanted = group_sum(jnp.where(mine, pair_orbital, 0), ("band",))
    first_owned = lax.axis_index("band") * local_count
    slots = jnp.zeros(wanted.shape + j_coeff.shape[1:], jnp.float32)
    for number in range(local_count):
        hit = (wanted == first_owned + number)[:, :, None, None, None]
        slots = jnp.where(hit, j_coeff[number][None, None], slots)
    arrived = lax.all_to_all(slots, "band", 0, 0, tiled=True)
    own_orbital = synthesize(extended(i_coeff, sides, 8))[0]
    partner = synthesize(extended(jnp.sum(arrived, axis=0), sides, 8))
    density = own_orbital[None] * partner
    potential, energy_part = potentials(density)
    weights = pair_occ[0].astype(jnp.float32)
    applied = -jnp.sum(weights[:, None, None, None] * potential * partner, axis=0)
    length = own_orbital.shape[2]
    energy = energy_part / float(length**3)
    return (applied[None], energy[None])


def solution(mesh):
    in_specs = (
        P("band", "gy", "gz", None),
        P("band", "gy", "gz", None),
        P("band", None),
        P("band", None),
    )
    out_specs = (P("band", "gy", "gz", None), P("band", None))
    return jax.shard_map(shards, mesh=mesh, in_specs=in_specs, out_specs=out_specs, check_vma=False)
```

```python
import math

import jax
import jax.numpy as jnp
import numpy as np
from jax import lax
from jax.sharding import PartitionSpec as P

tap_offsets = np.arange(-8, 8)
raw_taps = 0.6 ** np.abs(tap_offsets + 0.5) * np.where(tap_offsets % 2 == 0, 1.0, -0.6)
FILTER_TAPS = raw_taps / np.sqrt(np.sum(raw_taps**2))
SCREEN = 0.001
precise_mode = lax.Precision.HIGHEST
fast_mode = lax.Precision.HIGH


def extended(cells, sides, width):
    for axis, dim in sides:
        count = lax.axis_size(axis)
        extent = cells.shape[dim]
        head = lax.slice_in_dim(cells, 0, width, axis=dim)
        tail = lax.slice_in_dim(cells, extent - width, extent, axis=dim)
        if count == 2:
            first = lax.axis_index(axis) == 0
            got = lax.ppermute(jnp.where(first, tail, head), axis, [(0, 1), (1, 0)])
            empty = jnp.zeros_like(got)
            before = jnp.where(first, empty, got)
            after = jnp.where(first, got, empty)
        else:
            before = lax.ppermute(tail, axis, [(i, i + 1) for i in range(count - 1)])
            after = lax.ppermute(head, axis, [(i + 1, i) for i in range(count - 1)])
        cells = jnp.concatenate([before, cells, after], axis=dim)
    return cells


def group_sum(values, axes):
    total = values
    for axis in axes:
        count = lax.axis_size(axis)
        if count & (count - 1):
            total = lax.psum(total, axis)
            continue
        step = 1
        while step < count:
            total = total + lax.ppermute(total, axis, [(i, i ^ step) for i in range(count)])
            step *= 2
    return total


def band_matrix(row_count, col_count, shift_by):
    row_index = jnp.arange(row_count, dtype=jnp.int32)[:, None]
    col_index = jnp.arange(col_count, dtype=jnp.int32)[None, :]
    offset = row_index - shift_by - col_index
    picked = jnp.zeros((row_count, col_count), jnp.float32)
    for number in range(16):
        picked = picked + jnp.where(offset == number - 8, float(FILTER_TAPS[number]), 0.0)
    return picked


def synthesize(padded):
    wide_y, wide_z, length = (padded.shape[1], padded.shape[2], padded.shape[3])
    matrix_y = band_matrix(wide_y, wide_y - 16, 8)
    matrix_z = band_matrix(wide_z, wide_z - 16, 8)
    matrix_x = band_matrix(length, length, 0)
    step_one = jnp.matmul(padded, matrix_x, precision=precise_mode)
    step_two = jnp.einsum("oyqx,qz->oyzx", step_one, matrix_z, precision=precise_mode)
    return jnp.einsum("oqzx,qy->oyzx", step_two, matrix_y, precision=precise_mode)


def channel_of(channel, length):
    period = 2 * length
    frequency = jnp.where(channel <= length, channel, channel - length)
    angles = 2.0 * math.pi / period * (frequency % period).astype(jnp.float32)
    lattice = 2.0 - 2.0 * jnp.cos(angles)
    fold = jnp.where((channel == 0) | (channel == length), 1.0, 2.0)
    return frequency, lattice, fold


def channel_table(length):
    period = 2 * length
    channel = jnp.arange(period, dtype=jnp.int32)[None, :]
    frequency, _, _ = channel_of(channel, length)
    positions = jnp.arange(length, dtype=jnp.int32)[:, None] * frequency
    angles = 2.0 * math.pi / period * (positions % period).astype(jnp.float32)
    return jnp.where(channel <= length, jnp.cos(angles), jnp.sin(angles))


def contract(left, right, left_dim, right_dim):
    return lax.dot_general(
        left, right, (((left_dim,), (right_dim,)), ((), ())), precision=fast_mode
    )


def potentials(density):
    pair_count, rows_y, rows_z, length = density.shape
    period = 2 * length
    count_y = lax.axis_size("gy")
    count_z = lax.axis_size("gz")
    spread = count_y * count_z
    width = period // spread
    table = channel_table(length)
    flat = density.transpose(0, 2, 1, 3).reshape(pair_count * rows_y * rows_z, length)
    along_x = contract(table, flat, 0, 1)
    send = along_x.reshape(spread, width, pair_count, rows_y * rows_z)
    got = lax.all_to_all(send, ("gy", "gz"), 0, 0, tiled=True)
    got = got.reshape(count_y, count_z, width, pair_count, rows_z, rows_y)
    got = got.transpose(2, 3, 1, 4, 0, 5).reshape(
        width, pair_count, count_z * rows_z, count_y * rows_y
    )
    along_z = contract(got, table, 3, 0)
    spectrum = contract(along_z, table, 2, 0)
    own = lax.axis_index(("gy", "gz")) * width + jnp.arange(width, dtype=jnp.int32)
    _, lattice_x, fold_x = channel_of(own, length)
    _, lattice_all, fold_all = channel_of(jnp.arange(period, dtype=jnp.int32), length)
    weight = (
        fold_x[:, None, None] * fold_all[None, :, None] * fold_all[None, None, :]
    ) / (
        (lattice_x[:, None, None] + lattice_all[None, :, None] + lattice_all[None, None, :] + SCREEN)
        * float(period**3)
    )
    weighted = spectrum * weight[:, None]
    energy_part = jnp.sum(weighted * spectrum, axis=(0, 2, 3))
    back_y = contract(weighted, table, 3, 1)
    back_z = contract(back_y, table, 2, 1)
    back = back_z.reshape(width, pair_count, count_z, rows_z, count_y, rows_y)
    back = back.transpose(4, 2, 0, 1, 3, 5).reshape(spread, width, pair_count, rows_y * rows_z)
    rounds = [
        (axis, 1 << bit)
        for axis in ("gz", "gy")
        for bit in range(lax.axis_size(axis).bit_length() - 1)
    ]
    if rounds and all(lax.axis_size(axis) & (lax.axis_size(axis) - 1) == 0 for axis in ("gz", "gy")):
        energy_total = energy_part
        for number, (axis, step) in enumerate(rounds):
            count = lax.axis_size(axis)
            energy_total = energy_total + lax.ppermute(
                energy_total, axis, [(i, i ^ step) for i in range(count)]
            )
            if number == 0:
                back, energy_total = lax.optimization_barrier((back, energy_total))
    else:
        energy_total = group_sum(energy_part, ("gz", "gy"))
    got = lax.all_to_all(back, ("gy", "gz"), 0, 0, tiled=True)
    got = got.reshape(period, pair_count, rows_y * rows_z)
    result = contract(got, table, 0, 1)
    result = result.reshape(pair_count, rows_z, rows_y, length).transpose(0, 2, 1, 3)
    return result, energy_total


def shards(i_coeff, j_coeff, pair_orbital, pair_occ):
    sides = (("gy", 1), ("gz", 2))
    local_count = j_coeff.shape[0]
    band_count = lax.axis_size("band")
    mine = lax.axis_index("band") == jnp.arange(band_count, dtype=jnp.int32)[:, None]
    wanted = group_sum(jnp.where(mine, pair_orbital, 0), ("band",))
    first_owned = lax.axis_index("band") * local_count
    slots = jnp.zeros(wanted.shape + j_coeff.shape[1:], jnp.float32)
    for number in range(local_count):
        hit = (wanted == first_owned + number)[:, :, None, None, None]
        slots = jnp.where(hit, j_coeff[number][None, None], slots)
    arrived = lax.all_to_all(slots, "band", 0, 0, tiled=True)
    own_orbital = synthesize(extended(i_coeff, sides, 8))[0]
    partner = synthesize(extended(jnp.sum(arrived, axis=0), sides, 8))
    density = own_orbital[None] * partner
    potential, energy_part = potentials(density)
    weights = pair_occ[0].astype(jnp.float32)
    applied = -jnp.sum(weights[:, None, None, None] * potential * partner, axis=0)
    length = own_orbital.shape[2]
    energy = energy_part / float(length**3)
    return (applied[None], energy[None])


def solution(mesh):
    in_specs = (
        P("band", "gy", "gz", None),
        P("band", "gy", "gz", None),
        P("band", None),
        P("band", None),
    )
    out_specs = (P("band", "gy", "gz", None), P("band", None))
    return jax.shard_map(shards, mesh=mesh, in_specs=in_specs, out_specs=out_specs, check_vma=False)
```

```python
import math

import jax
import jax.numpy as jnp
import numpy as np
from jax import lax
from jax.sharding import PartitionSpec as P

tap_offsets = np.arange(-8, 8)
raw_taps = 0.6 ** np.abs(tap_offsets + 0.5) * np.where(tap_offsets % 2 == 0, 1.0, -0.6)
FILTER_TAPS = raw_taps / np.sqrt(np.sum(raw_taps**2))
SCREEN = 0.001
precise_mode = lax.Precision.HIGHEST
fast_mode = lax.Precision.HIGH


def extended(cells, sides, width):
    for axis, dim in sides:
        count = lax.axis_size(axis)
        extent = cells.shape[dim]
        head = lax.slice_in_dim(cells, 0, width, axis=dim)
        tail = lax.slice_in_dim(cells, extent - width, extent, axis=dim)
        if count == 2:
            first = lax.axis_index(axis) == 0
            got = lax.ppermute(jnp.where(first, tail, head), axis, [(0, 1), (1, 0)])
            empty = jnp.zeros_like(got)
            before = jnp.where(first, empty, got)
            after = jnp.where(first, got, empty)
        else:
            before = lax.ppermute(tail, axis, [(i, i + 1) for i in range(count - 1)])
            after = lax.ppermute(head, axis, [(i + 1, i) for i in range(count - 1)])
        cells = jnp.concatenate([before, cells, after], axis=dim)
    return cells


def group_sum(values, axes):
    total = values
    for axis in axes:
        count = lax.axis_size(axis)
        if count & (count - 1):
            total = lax.psum(total, axis)
            continue
        step = 1
        while step < count:
            total = total + lax.ppermute(total, axis, [(i, i ^ step) for i in range(count)])
            step *= 2
    return total


def band_matrix(row_count, col_count, shift_by):
    row_index = jnp.arange(row_count, dtype=jnp.int32)[:, None]
    col_index = jnp.arange(col_count, dtype=jnp.int32)[None, :]
    offset = row_index - shift_by - col_index
    picked = jnp.zeros((row_count, col_count), jnp.float32)
    for number in range(16):
        picked = picked + jnp.where(offset == number - 8, float(FILTER_TAPS[number]), 0.0)
    return picked


def synthesize(padded):
    wide_y, wide_z, length = (padded.shape[1], padded.shape[2], padded.shape[3])
    matrix_y = band_matrix(wide_y, wide_y - 16, 8)
    matrix_z = band_matrix(wide_z, wide_z - 16, 8)
    matrix_x = band_matrix(length, length, 0)
    step_one = jnp.matmul(padded, matrix_x, precision=precise_mode)
    step_two = jnp.einsum("oyqx,qz->oyzx", step_one, matrix_z, precision=precise_mode)
    return jnp.einsum("oqzx,qy->oyzx", step_two, matrix_y, precision=precise_mode)


def channel_of(channel, length):
    period = 2 * length
    frequency = jnp.where(channel <= length, channel, channel - length)
    angles = 2.0 * math.pi / period * (frequency % period).astype(jnp.float32)
    lattice = 2.0 - 2.0 * jnp.cos(angles)
    fold = jnp.where((channel == 0) | (channel == length), 1.0, 2.0)
    return frequency, lattice, fold


def channel_table(length):
    period = 2 * length
    channel = jnp.arange(period, dtype=jnp.int32)[None, :]
    frequency, _, _ = channel_of(channel, length)
    positions = jnp.arange(length, dtype=jnp.int32)[:, None] * frequency
    angles = 2.0 * math.pi / period * (positions % period).astype(jnp.float32)
    return jnp.where(channel <= length, jnp.cos(angles), jnp.sin(angles))


def contract(left, right, left_dim, right_dim):
    return lax.dot_general(
        left, right, (((left_dim,), (right_dim,)), ((), ())), precision=fast_mode
    )


def potentials(density):
    pair_count, rows_y, rows_z, length = density.shape
    period = 2 * length
    count_y = lax.axis_size("gy")
    count_z = lax.axis_size("gz")
    spread = count_y * count_z
    width = period // spread
    table = channel_table(length)
    flat = density.transpose(0, 2, 1, 3).reshape(pair_count * rows_y * rows_z, length)
    along_x = contract(table, flat, 0, 1)
    send = along_x.reshape(spread, width, pair_count, rows_y * rows_z)
    got = lax.all_to_all(send, ("gy", "gz"), 0, 0, tiled=True)
    got = got.reshape(count_y, count_z, width, pair_count, rows_z, rows_y)
    table_y = table.reshape(count_y, rows_y, period)
    along_y = contract(got[0], table_y[0], 4, 0)
    for part in range(1, count_y):
        along_y = along_y + contract(got[part], table_y[part], 4, 0)
    table_z = table.reshape(count_z, rows_z, period)
    spectrum = contract(along_y[0], table_z[0], 2, 0)
    for part in range(1, count_z):
        spectrum = spectrum + contract(along_y[part], table_z[part], 2, 0)
    own = lax.axis_index(("gy", "gz")) * width + jnp.arange(width, dtype=jnp.int32)
    _, lattice_x, fold_x = channel_of(own, length)
    _, lattice_all, fold_all = channel_of(jnp.arange(period, dtype=jnp.int32), length)
    weight = (
        fold_x[:, None, None] * fold_all[None, :, None] * fold_all[None, None, :]
    ) / (
        (lattice_x[:, None, None] + lattice_all[None, :, None] + lattice_all[None, None, :] + SCREEN)
        * float(period**3)
    )
    weighted = spectrum * weight[:, None]
    energy_part = jnp.sum(weighted * spectrum, axis=(0, 2, 3))
    back_y = contract(weighted, table, 3, 1)
    back_z = contract(back_y, table, 2, 1)
    back = back_z.reshape(width, pair_count, count_z, rows_z, count_y, rows_y)
    back = back.transpose(4, 2, 0, 1, 3, 5).reshape(spread, width, pair_count, rows_y * rows_z)
    energy_total = group_sum(energy_part, ("gz", "gy"))
    got = lax.all_to_all(back, ("gy", "gz"), 0, 0, tiled=True)
    got = got.reshape(period, pair_count, rows_y * rows_z)
    result = contract(got, table, 0, 1)
    result = result.reshape(pair_count, rows_z, rows_y, length).transpose(0, 2, 1, 3)
    return result, energy_total


def shards(i_coeff, j_coeff, pair_orbital, pair_occ):
    sides = (("gy", 1), ("gz", 2))
    local_count = j_coeff.shape[0]
    band_count = lax.axis_size("band")
    mine = lax.axis_index("band") == jnp.arange(band_count, dtype=jnp.int32)[:, None]
    wanted = group_sum(jnp.where(mine, pair_orbital, 0), ("band",))
    first_owned = lax.axis_index("band") * local_count
    slots = jnp.zeros(wanted.shape + j_coeff.shape[1:], jnp.float32)
    for number in range(local_count):
        hit = (wanted == first_owned + number)[:, :, None, None, None]
        slots = jnp.where(hit, j_coeff[number][None, None], slots)
    arrived = lax.all_to_all(slots, "band", 0, 0, tiled=True)
    own_orbital = synthesize(extended(i_coeff, sides, 8))[0]
    partner = synthesize(extended(jnp.sum(arrived, axis=0), sides, 8))
    density = own_orbital[None] * partner
    potential, energy_part = potentials(density)
    weights = pair_occ[0].astype(jnp.float32)
    applied = -jnp.sum(weights[:, None, None, None] * potential * partner, axis=0)
    length = own_orbital.shape[2]
    energy = energy_part / float(length**3)
    return (applied[None], energy[None])


def solution(mesh):
    in_specs = (
        P("band", "gy", "gz", None),
        P("band", "gy", "gz", None),
        P("band", None),
        P("band", None),
    )
    out_specs = (P("band", "gy", "gz", None), P("band", None))
    return jax.shard_map(shards, mesh=mesh, in_specs=in_specs, out_specs=out_specs, check_vma=False)
```

```python
import math

import jax
import jax.numpy as jnp
import numpy as np
from jax import lax
from jax.sharding import PartitionSpec as P

tap_offsets = np.arange(-8, 8)
raw_taps = 0.6 ** np.abs(tap_offsets + 0.5) * np.where(tap_offsets % 2 == 0, 1.0, -0.6)
FILTER_TAPS = raw_taps / np.sqrt(np.sum(raw_taps**2))
SCREEN = 0.001
precise_mode = lax.Precision.HIGHEST
fast_mode = lax.Precision.HIGH


def extended(cells, sides, width):
    for axis, dim in sides:
        count = lax.axis_size(axis)
        extent = cells.shape[dim]
        head = lax.slice_in_dim(cells, 0, width, axis=dim)
        tail = lax.slice_in_dim(cells, extent - width, extent, axis=dim)
        if count == 2:
            first = lax.axis_index(axis) == 0
            got = lax.ppermute(jnp.where(first, tail, head), axis, [(0, 1), (1, 0)])
            empty = jnp.zeros_like(got)
            before = jnp.where(first, empty, got)
            after = jnp.where(first, got, empty)
        else:
            before = lax.ppermute(tail, axis, [(i, i + 1) for i in range(count - 1)])
            after = lax.ppermute(head, axis, [(i + 1, i) for i in range(count - 1)])
        cells = jnp.concatenate([before, cells, after], axis=dim)
    return cells


def group_sum(values, axes):
    total = values
    for axis in axes:
        count = lax.axis_size(axis)
        if count & (count - 1):
            total = lax.psum(total, axis)
            continue
        step = 1
        while step < count:
            total = total + lax.ppermute(total, axis, [(i, i ^ step) for i in range(count)])
            step *= 2
    return total


def band_matrix(row_count, col_count, shift_by):
    row_index = jnp.arange(row_count, dtype=jnp.int32)[:, None]
    col_index = jnp.arange(col_count, dtype=jnp.int32)[None, :]
    offset = row_index - shift_by - col_index
    picked = jnp.zeros((row_count, col_count), jnp.float32)
    for number in range(16):
        picked = picked + jnp.where(offset == number - 8, float(FILTER_TAPS[number]), 0.0)
    return picked


def synthesize(padded):
    wide_y, wide_z, length = (padded.shape[1], padded.shape[2], padded.shape[3])
    matrix_y = band_matrix(wide_y, wide_y - 16, 8)
    matrix_z = band_matrix(wide_z, wide_z - 16, 8)
    matrix_x = band_matrix(length, length, 0)
    step_one = jnp.matmul(padded, matrix_x, precision=precise_mode)
    step_two = jnp.einsum("oyqx,qz->oyzx", step_one, matrix_z, precision=precise_mode)
    return jnp.einsum("oqzx,qy->oyzx", step_two, matrix_y, precision=precise_mode)


def channel_of(channel, length):
    period = 2 * length
    frequency = jnp.where(channel <= length, channel, channel - length)
    angles = 2.0 * math.pi / period * (frequency % period).astype(jnp.float32)
    lattice = 2.0 - 2.0 * jnp.cos(angles)
    fold = jnp.where((channel == 0) | (channel == length), 1.0, 2.0)
    return frequency, lattice, fold


def channel_table(length):
    period = 2 * length
    channel = jnp.arange(period, dtype=jnp.int32)[None, :]
    frequency, _, _ = channel_of(channel, length)
    positions = jnp.arange(length, dtype=jnp.int32)[:, None] * frequency
    angles = 2.0 * math.pi / period * (positions % period).astype(jnp.float32)
    return jnp.where(channel <= length, jnp.cos(angles), jnp.sin(angles))


def contract(left, right, left_dim, right_dim):
    return lax.dot_general(
        left, right, (((left_dim,), (right_dim,)), ((), ())), precision=fast_mode
    )


def potentials(density):
    pair_count, rows_y, rows_z, length = density.shape
    period = 2 * length
    count_y = lax.axis_size("gy")
    count_z = lax.axis_size("gz")
    spread = count_y * count_z
    width = period // spread
    table = channel_table(length)
    flat = density.transpose(0, 2, 1, 3).reshape(pair_count * rows_y * rows_z, length)
    along_x = contract(table, flat, 0, 1)
    send = along_x.reshape(spread, width, pair_count, rows_y * rows_z)
    got = lax.all_to_all(send, ("gy", "gz"), 0, 0, tiled=True)
    got = got.reshape(count_y, count_z, width, pair_count, rows_z, rows_y)
    table_y = table.reshape(count_y, rows_y, period)
    along_y = contract(got[0], table_y[0], 4, 0)
    for part in range(1, count_y):
        along_y = along_y + contract(got[part], table_y[part], 4, 0)
    along_y = along_y.transpose(1, 2, 0, 3, 4).reshape(width, pair_count, count_z * rows_z, period)
    spectrum = contract(along_y, table, 2, 0)
    own = lax.axis_index(("gy", "gz")) * width + jnp.arange(width, dtype=jnp.int32)
    _, lattice_x, fold_x = channel_of(own, length)
    _, lattice_all, fold_all = channel_of(jnp.arange(period, dtype=jnp.int32), length)
    weight = (
        fold_x[:, None, None] * fold_all[None, :, None] * fold_all[None, None, :]
    ) / (
        (lattice_x[:, None, None] + lattice_all[None, :, None] + lattice_all[None, None, :] + SCREEN)
        * float(period**3)
    )
    weighted = spectrum * weight[:, None]
    energy_part = jnp.sum(weighted * spectrum, axis=(0, 2, 3))
    back_y = contract(weighted, table, 3, 1)
    back_z = contract(back_y, table, 2, 1)
    back = back_z.reshape(width, pair_count, count_z, rows_z, count_y, rows_y)
    back = back.transpose(4, 2, 0, 1, 3, 5).reshape(spread, width, pair_count, rows_y * rows_z)
    energy_total = group_sum(energy_part, ("gz", "gy"))
    got = lax.all_to_all(back, ("gy", "gz"), 0, 0, tiled=True)
    got = got.reshape(period, pair_count, rows_y * rows_z)
    result = contract(got, table, 0, 1)
    result = result.reshape(pair_count, rows_z, rows_y, length).transpose(0, 2, 1, 3)
    return result, energy_total


def shards(i_coeff, j_coeff, pair_orbital, pair_occ):
    sides = (("gy", 1), ("gz", 2))
    local_count = j_coeff.shape[0]
    band_count = lax.axis_size("band")
    mine = lax.axis_index("band") == jnp.arange(band_count, dtype=jnp.int32)[:, None]
    wanted = group_sum(jnp.where(mine, pair_orbital, 0), ("band",))
    first_owned = lax.axis_index("band") * local_count
    slots = jnp.zeros(wanted.shape + j_coeff.shape[1:], jnp.float32)
    for number in range(local_count):
        hit = (wanted == first_owned + number)[:, :, None, None, None]
        slots = jnp.where(hit, j_coeff[number][None, None], slots)
    arrived = lax.all_to_all(slots, "band", 0, 0, tiled=True)
    own_orbital = synthesize(extended(i_coeff, sides, 8))[0]
    partner = synthesize(extended(jnp.sum(arrived, axis=0), sides, 8))
    density = own_orbital[None] * partner
    potential, energy_part = potentials(density)
    weights = pair_occ[0].astype(jnp.float32)
    applied = -jnp.sum(weights[:, None, None, None] * potential * partner, axis=0)
    length = own_orbital.shape[2]
    energy = energy_part / float(length**3)
    return (applied[None], energy[None])


def solution(mesh):
    in_specs = (
        P("band", "gy", "gz", None),
        P("band", "gy", "gz", None),
        P("band", None),
        P("band", None),
    )
    out_specs = (P("band", "gy", "gz", None), P("band", None))
    return jax.shard_map(shards, mesh=mesh, in_specs=in_specs, out_specs=out_specs, check_vma=False)
```

```python
import math

import jax
import jax.numpy as jnp
import numpy as np
from jax import lax
from jax.sharding import PartitionSpec as P

tap_offsets = np.arange(-8, 8)
raw_taps = 0.6 ** np.abs(tap_offsets + 0.5) * np.where(tap_offsets % 2 == 0, 1.0, -0.6)
FILTER_TAPS = raw_taps / np.sqrt(np.sum(raw_taps**2))
SCREEN = 0.001
precise_mode = lax.Precision.HIGHEST
fast_mode = lax.Precision.HIGH


def extended(cells, sides, width):
    for axis, dim in sides:
        count = lax.axis_size(axis)
        extent = cells.shape[dim]
        head = lax.slice_in_dim(cells, 0, width, axis=dim)
        tail = lax.slice_in_dim(cells, extent - width, extent, axis=dim)
        if count == 2:
            first = lax.axis_index(axis) == 0
            got = lax.ppermute(jnp.where(first, tail, head), axis, [(0, 1), (1, 0)])
            empty = jnp.zeros_like(got)
            before = jnp.where(first, empty, got)
            after = jnp.where(first, got, empty)
        else:
            before = lax.ppermute(tail, axis, [(i, i + 1) for i in range(count - 1)])
            after = lax.ppermute(head, axis, [(i + 1, i) for i in range(count - 1)])
        cells = jnp.concatenate([before, cells, after], axis=dim)
    return cells


def group_sum(values, axes):
    total = values
    for axis in axes:
        count = lax.axis_size(axis)
        if count & (count - 1):
            total = lax.psum(total, axis)
            continue
        step = 1
        while step < count:
            total = total + lax.ppermute(total, axis, [(i, i ^ step) for i in range(count)])
            step *= 2
    return total


def band_matrix(row_count, col_count, shift_by):
    row_index = jnp.arange(row_count, dtype=jnp.int32)[:, None]
    col_index = jnp.arange(col_count, dtype=jnp.int32)[None, :]
    offset = row_index - shift_by - col_index
    picked = jnp.zeros((row_count, col_count), jnp.float32)
    for number in range(16):
        picked = picked + jnp.where(offset == number - 8, float(FILTER_TAPS[number]), 0.0)
    return picked


def synthesize(padded):
    wide_y, wide_z, length = (padded.shape[1], padded.shape[2], padded.shape[3])
    matrix_y = band_matrix(wide_y, wide_y - 16, 8)
    matrix_z = band_matrix(wide_z, wide_z - 16, 8)
    matrix_x = band_matrix(length, length, 0)
    step_one = jnp.matmul(padded, matrix_x, precision=precise_mode)
    step_two = jnp.einsum("oyqx,qz->oyzx", step_one, matrix_z, precision=precise_mode)
    return jnp.einsum("oqzx,qy->oyzx", step_two, matrix_y, precision=precise_mode)


def channel_of(channel, length):
    period = 2 * length
    frequency = jnp.where(channel <= length, channel, channel - length)
    angles = 2.0 * math.pi / period * (frequency % period).astype(jnp.float32)
    lattice = 2.0 - 2.0 * jnp.cos(angles)
    fold = jnp.where((channel == 0) | (channel == length), 1.0, 2.0)
    return frequency, lattice, fold


def channel_table(length):
    period = 2 * length
    channel = jnp.arange(period, dtype=jnp.int32)[None, :]
    frequency, _, _ = channel_of(channel, length)
    positions = jnp.arange(length, dtype=jnp.int32)[:, None] * frequency
    angles = 2.0 * math.pi / period * (positions % period).astype(jnp.float32)
    return jnp.where(channel <= length, jnp.cos(angles), jnp.sin(angles))


def contract(left, right, left_dim, right_dim):
    return lax.dot_general(
        left, right, (((left_dim,), (right_dim,)), ((), ())), precision=fast_mode
    )


def channel_weight(length):
    period = 2 * length
    width = period // (lax.axis_size("gy") * lax.axis_size("gz"))
    own = lax.axis_index(("gy", "gz")) * width + jnp.arange(width, dtype=jnp.int32)
    _, lattice_x, fold_x = channel_of(own, length)
    _, lattice_all, fold_all = channel_of(jnp.arange(period, dtype=jnp.int32), length)
    weight = (
        fold_x[:, None, None] * fold_all[None, :, None] * fold_all[None, None, :]
    ) / (
        (lattice_x[:, None, None] + lattice_all[None, :, None] + lattice_all[None, None, :] + SCREEN)
        * float(period**3)
    )
    return weight


def potentials(density, weight):
    pair_count, rows_y, rows_z, length = density.shape
    period = 2 * length
    count_y = lax.axis_size("gy")
    count_z = lax.axis_size("gz")
    spread = count_y * count_z
    width = period // spread
    table = channel_table(length)
    flat = density.transpose(0, 2, 1, 3).reshape(pair_count * rows_y * rows_z, length)
    along_x = contract(table, flat, 0, 1)
    send = along_x.reshape(spread, width, pair_count, rows_y * rows_z)
    got = lax.all_to_all(send, ("gy", "gz"), 0, 0, tiled=True)
    got = got.reshape(count_y, count_z, width, pair_count, rows_z, rows_y)
    table_y = table.reshape(count_y, rows_y, period)
    along_y = contract(got[0], table_y[0], 4, 0)
    for part in range(1, count_y):
        along_y = along_y + contract(got[part], table_y[part], 4, 0)
    along_y = along_y.transpose(1, 2, 0, 3, 4).reshape(width, pair_count, count_z * rows_z, period)
    spectrum = contract(along_y, table, 2, 0)
    weighted = spectrum * weight[:, None]
    energy_part = jnp.sum(weighted * spectrum, axis=(0, 2, 3))
    back_y = contract(weighted, table, 3, 1)
    back_z = contract(back_y, table, 2, 1)
    back = back_z.reshape(width, pair_count, count_z, rows_z, count_y, rows_y)
    back = back.transpose(4, 2, 0, 1, 3, 5).reshape(spread, width, pair_count, rows_y * rows_z)
    energy_total = group_sum(energy_part, ("gz", "gy"))
    got = lax.all_to_all(back, ("gy", "gz"), 0, 0, tiled=True)
    got = got.reshape(period, pair_count, rows_y * rows_z)
    result = contract(got, table, 0, 1)
    result = result.reshape(pair_count, rows_z, rows_y, length).transpose(0, 2, 1, 3)
    return result, energy_total


def shards(i_coeff, j_coeff, pair_orbital, pair_occ):
    sides = (("gy", 1), ("gz", 2))
    local_count = j_coeff.shape[0]
    band_count = lax.axis_size("band")
    mine = lax.axis_index("band") == jnp.arange(band_count, dtype=jnp.int32)[:, None]
    wanted = group_sum(jnp.where(mine, pair_orbital, 0), ("band",))
    first_owned = lax.axis_index("band") * local_count
    slots = jnp.zeros(wanted.shape + j_coeff.shape[1:], jnp.float32)
    for number in range(local_count):
        hit = (wanted == first_owned + number)[:, :, None, None, None]
        slots = jnp.where(hit, j_coeff[number][None, None], slots)
    arrived = lax.all_to_all(slots, "band", 0, 0, tiled=True)
    arrived, weight = lax.optimization_barrier((arrived, channel_weight(j_coeff.shape[3])))
    own_orbital = synthesize(extended(i_coeff, sides, 8))[0]
    partner = synthesize(extended(jnp.sum(arrived, axis=0), sides, 8))
    density = own_orbital[None] * partner
    potential, energy_part = potentials(density, weight)
    weights = pair_occ[0].astype(jnp.float32)
    applied = -jnp.sum(weights[:, None, None, None] * potential * partner, axis=0)
    length = own_orbital.shape[2]
    energy = energy_part / float(length**3)
    return (applied[None], energy[None])


def solution(mesh):
    in_specs = (
        P("band", "gy", "gz", None),
        P("band", "gy", "gz", None),
        P("band", None),
        P("band", None),
    )
    out_specs = (P("band", "gy", "gz", None), P("band", None))
    return jax.shard_map(shards, mesh=mesh, in_specs=in_specs, out_specs=out_specs, check_vma=False)
```

```python
import math

import jax
import jax.numpy as jnp
import numpy as np
from jax import lax
from jax.sharding import PartitionSpec as P

tap_offsets = np.arange(-8, 8)
raw_taps = 0.6 ** np.abs(tap_offsets + 0.5) * np.where(tap_offsets % 2 == 0, 1.0, -0.6)
FILTER_TAPS = raw_taps / np.sqrt(np.sum(raw_taps**2))
SCREEN = 0.001
precise_mode = lax.Precision.HIGHEST
fast_mode = lax.Precision.HIGH


def extended(cells, sides, width):
    for axis, dim in sides:
        count = lax.axis_size(axis)
        extent = cells.shape[dim]
        head = lax.slice_in_dim(cells, 0, width, axis=dim)
        tail = lax.slice_in_dim(cells, extent - width, extent, axis=dim)
        if count == 2:
            first = lax.axis_index(axis) == 0
            got = lax.ppermute(jnp.where(first, tail, head), axis, [(0, 1), (1, 0)])
            empty = jnp.zeros_like(got)
            before = jnp.where(first, empty, got)
            after = jnp.where(first, got, empty)
        else:
            before = lax.ppermute(tail, axis, [(i, i + 1) for i in range(count - 1)])
            after = lax.ppermute(head, axis, [(i + 1, i) for i in range(count - 1)])
        cells = jnp.concatenate([before, cells, after], axis=dim)
    return cells


def group_sum(values, axes):
    total = values
    for axis in axes:
        count = lax.axis_size(axis)
        if count & (count - 1):
            total = lax.psum(total, axis)
            continue
        step = 1
        while step < count:
            total = total + lax.ppermute(total, axis, [(i, i ^ step) for i in range(count)])
            step *= 2
    return total


def band_matrix(row_count, col_count, shift_by):
    row_index = jnp.arange(row_count, dtype=jnp.int32)[:, None]
    col_index = jnp.arange(col_count, dtype=jnp.int32)[None, :]
    offset = row_index - shift_by - col_index
    picked = jnp.zeros((row_count, col_count), jnp.float32)
    for number in range(16):
        picked = picked + jnp.where(offset == number - 8, float(FILTER_TAPS[number]), 0.0)
    return picked


def synthesize(padded):
    wide_y, wide_z, length = (padded.shape[1], padded.shape[2], padded.shape[3])
    matrix_y = band_matrix(wide_y, wide_y - 16, 8)
    matrix_z = band_matrix(wide_z, wide_z - 16, 8)
    matrix_x = band_matrix(length, length, 0)
    step_one = jnp.matmul(padded, matrix_x, precision=precise_mode)
    step_two = jnp.einsum("oyqx,qz->oyzx", step_one, matrix_z, precision=precise_mode)
    return jnp.einsum("oqzx,qy->oyzx", step_two, matrix_y, precision=precise_mode)


def channel_of(channel, length):
    period = 2 * length
    frequency = jnp.where(channel <= length, channel, channel - length)
    angles = 2.0 * math.pi / period * (frequency % period).astype(jnp.float32)
    lattice = 2.0 - 2.0 * jnp.cos(angles)
    fold = jnp.where((channel == 0) | (channel == length), 1.0, 2.0)
    return frequency, lattice, fold


def channel_table(length):
    period = 2 * length
    channel = jnp.arange(period, dtype=jnp.int32)[None, :]
    frequency, _, _ = channel_of(channel, length)
    positions = jnp.arange(length, dtype=jnp.int32)[:, None] * frequency
    angles = 2.0 * math.pi / period * (positions % period).astype(jnp.float32)
    return jnp.where(channel <= length, jnp.cos(angles), jnp.sin(angles))


def contract(left, right, left_dim, right_dim):
    return lax.dot_general(
        left, right, (((left_dim,), (right_dim,)), ((), ())), precision=fast_mode
    )


def channel_weight(length):
    period = 2 * length
    width = period // (lax.axis_size("gy") * lax.axis_size("gz"))
    own = lax.axis_index(("gy", "gz")) * width + jnp.arange(width, dtype=jnp.int32)
    _, lattice_x, fold_x = channel_of(own, length)
    _, lattice_all, fold_all = channel_of(jnp.arange(period, dtype=jnp.int32), length)
    weight = (
        fold_x[:, None, None] * fold_all[None, :, None] * fold_all[None, None, :]
    ) / (
        (lattice_x[:, None, None] + lattice_all[None, :, None] + lattice_all[None, None, :] + SCREEN)
        * float(period**3)
    )
    return weight


def potentials(density, weight):
    pair_count, rows_y, rows_z, length = density.shape
    period = 2 * length
    count_y = lax.axis_size("gy")
    count_z = lax.axis_size("gz")
    spread = count_y * count_z
    width = period // spread
    table = channel_table(length)
    flat = density.transpose(0, 2, 1, 3).reshape(pair_count * rows_y * rows_z, length)
    along_x = contract(table, flat, 0, 1)
    send = along_x.reshape(spread, width, pair_count, rows_y * rows_z)
    got = lax.all_to_all(send, ("gy", "gz"), 0, 0, tiled=True)
    got = got.reshape(count_y, count_z, width, pair_count, rows_z, rows_y)
    table_y = table.reshape(count_y, rows_y, period)
    along_y = contract(got[0], table_y[0], 4, 0)
    for part in range(1, count_y):
        along_y = along_y + contract(got[part], table_y[part], 4, 0)
    along_y = along_y.transpose(1, 2, 0, 3, 4).reshape(width, pair_count, count_z * rows_z, period)
    spectrum = contract(along_y, table, 2, 0)
    weighted = spectrum * weight[:, None]
    energy_part = jnp.sum(weighted * spectrum, axis=(0, 2, 3))
    back_y = contract(weighted, table, 3, 1)
    back_z = contract(back_y, table, 2, 1)
    back = back_z.reshape(width, pair_count, count_z, rows_z, count_y, rows_y)
    back = back.transpose(4, 2, 0, 1, 3, 5).reshape(spread, width, pair_count, rows_y * rows_z)
    energy_total = group_sum(energy_part, ("gz", "gy"))
    got = lax.all_to_all(back, ("gy", "gz"), 0, 0, tiled=True)
    got = got.reshape(period, pair_count, rows_y * rows_z)
    result = contract(got, table, 0, 1)
    result = result.reshape(pair_count, rows_z, rows_y, length).transpose(0, 2, 1, 3)
    return result, energy_total


def shards(i_coeff, j_coeff, pair_orbital, pair_occ):
    sides = (("gy", 1), ("gz", 2))
    local_count = j_coeff.shape[0]
    band_count = lax.axis_size("band")
    mine = lax.axis_index("band") == jnp.arange(band_count, dtype=jnp.int32)[:, None]
    wanted = group_sum(jnp.where(mine, pair_orbital, 0), ("band",))
    first_owned = lax.axis_index("band") * local_count
    slots = jnp.zeros(wanted.shape + j_coeff.shape[1:], jnp.float32)
    for number in range(local_count):
        hit = (wanted == first_owned + number)[:, :, None, None, None]
        slots = jnp.where(hit, j_coeff[number][None, None], slots)
    arrived = lax.all_to_all(slots, "band", 0, 0, tiled=True)
    arrived, weight = lax.optimization_barrier((arrived, channel_weight(j_coeff.shape[3])))
    own_orbital = synthesize(extended(i_coeff, sides, 8))[0]
    partner = synthesize(extended(jnp.sum(arrived, axis=0), sides[::-1], 8))
    density = own_orbital[None] * partner
    potential, energy_part = potentials(density, weight)
    weights = pair_occ[0].astype(jnp.float32)
    applied = -jnp.sum(weights[:, None, None, None] * potential * partner, axis=0)
    length = own_orbital.shape[2]
    energy = energy_part / float(length**3)
    return (applied[None], energy[None])


def solution(mesh):
    in_specs = (
        P("band", "gy", "gz", None),
        P("band", "gy", "gz", None),
        P("band", None),
        P("band", None),
    )
    out_specs = (P("band", "gy", "gz", None), P("band", None))
    return jax.shard_map(shards, mesh=mesh, in_specs=in_specs, out_specs=out_specs, check_vma=False)
```

```python
import math

import jax
import jax.numpy as jnp
import numpy as np
from jax import lax
from jax.sharding import PartitionSpec as P

tap_offsets = np.arange(-8, 8)
raw_taps = 0.6 ** np.abs(tap_offsets + 0.5) * np.where(tap_offsets % 2 == 0, 1.0, -0.6)
FILTER_TAPS = raw_taps / np.sqrt(np.sum(raw_taps**2))
SCREEN = 0.001
precise_mode = lax.Precision.HIGHEST
fast_mode = lax.Precision.HIGH


def extended(cells, sides, width):
    for axis, dim in sides:
        count = lax.axis_size(axis)
        extent = cells.shape[dim]
        head = lax.slice_in_dim(cells, 0, width, axis=dim)
        tail = lax.slice_in_dim(cells, extent - width, extent, axis=dim)
        if count == 2:
            first = lax.axis_index(axis) == 0
            got = lax.ppermute(jnp.where(first, tail, head), axis, [(0, 1), (1, 0)])
            empty = jnp.zeros_like(got)
            before = jnp.where(first, empty, got)
            after = jnp.where(first, got, empty)
        else:
            before = lax.ppermute(tail, axis, [(i, i + 1) for i in range(count - 1)])
            after = lax.ppermute(head, axis, [(i + 1, i) for i in range(count - 1)])
        cells = jnp.concatenate([before, cells, after], axis=dim)
    return cells


def group_sum(values, axes):
    total = values
    for axis in axes:
        count = lax.axis_size(axis)
        if count & (count - 1):
            total = lax.psum(total, axis)
            continue
        step = 1
        while step < count:
            total = total + lax.ppermute(total, axis, [(i, i ^ step) for i in range(count)])
            step *= 2
    return total


def band_matrix(row_count, col_count, shift_by):
    row_index = jnp.arange(row_count, dtype=jnp.int32)[:, None]
    col_index = jnp.arange(col_count, dtype=jnp.int32)[None, :]
    offset = row_index - shift_by - col_index
    picked = jnp.zeros((row_count, col_count), jnp.float32)
    for number in range(16):
        picked = picked + jnp.where(offset == number - 8, float(FILTER_TAPS[number]), 0.0)
    return picked


def filter_x(cells):
    length = cells.shape[3]
    return jnp.matmul(cells, band_matrix(length, length, 0), precision=precise_mode)


def filter_yz(padded):
    wide_y, wide_z = padded.shape[1], padded.shape[2]
    matrix_y = band_matrix(wide_y, wide_y - 16, 8)
    matrix_z = band_matrix(wide_z, wide_z - 16, 8)
    step_one = jnp.einsum("oyqx,qz->oyzx", padded, matrix_z, precision=precise_mode)
    return jnp.einsum("oqzx,qy->oyzx", step_one, matrix_y, precision=precise_mode)


def synthesize(padded):
    wide_y, wide_z, length = (padded.shape[1], padded.shape[2], padded.shape[3])
    matrix_y = band_matrix(wide_y, wide_y - 16, 8)
    matrix_z = band_matrix(wide_z, wide_z - 16, 8)
    matrix_x = band_matrix(length, length, 0)
    step_one = jnp.matmul(padded, matrix_x, precision=precise_mode)
    step_two = jnp.einsum("oyqx,qz->oyzx", step_one, matrix_z, precision=precise_mode)
    return jnp.einsum("oqzx,qy->oyzx", step_two, matrix_y, precision=precise_mode)


def channel_of(channel, length):
    period = 2 * length
    frequency = jnp.where(channel <= length, channel, channel - length)
    angles = 2.0 * math.pi / period * (frequency % period).astype(jnp.float32)
    lattice = 2.0 - 2.0 * jnp.cos(angles)
    fold = jnp.where((channel == 0) | (channel == length), 1.0, 2.0)
    return frequency, lattice, fold


def channel_table(length):
    period = 2 * length
    channel = jnp.arange(period, dtype=jnp.int32)[None, :]
    frequency, _, _ = channel_of(channel, length)
    positions = jnp.arange(length, dtype=jnp.int32)[:, None] * frequency
    angles = 2.0 * math.pi / period * (positions % period).astype(jnp.float32)
    return jnp.where(channel <= length, jnp.cos(angles), jnp.sin(angles))


def contract(left, right, left_dim, right_dim):
    return lax.dot_general(
        left, right, (((left_dim,), (right_dim,)), ((), ())), precision=fast_mode
    )


def channel_weight(length):
    period = 2 * length
    width = period // (lax.axis_size("gy") * lax.axis_size("gz"))
    own = lax.axis_index(("gy", "gz")) * width + jnp.arange(width, dtype=jnp.int32)
    _, lattice_x, fold_x = channel_of(own, length)
    _, lattice_all, fold_all = channel_of(jnp.arange(period, dtype=jnp.int32), length)
    weight = (
        fold_x[:, None, None] * fold_all[None, :, None] * fold_all[None, None, :]
    ) / (
        (lattice_x[:, None, None] + lattice_all[None, :, None] + lattice_all[None, None, :] + SCREEN)
        * float(period**3)
    )
    return weight


def potentials(density, weight):
    pair_count, rows_y, rows_z, length = density.shape
    period = 2 * length
    count_y = lax.axis_size("gy")
    count_z = lax.axis_size("gz")
    spread = count_y * count_z
    width = period // spread
    table = channel_table(length)
    flat = density.transpose(0, 2, 1, 3).reshape(pair_count * rows_y * rows_z, length)
    along_x = contract(table, flat, 0, 1)
    send = along_x.reshape(spread, width, pair_count, rows_y * rows_z)
    got = lax.all_to_all(send, ("gy", "gz"), 0, 0, tiled=True)
    got = got.reshape(count_y, count_z, width, pair_count, rows_z, rows_y)
    table_y = table.reshape(count_y, rows_y, period)
    along_y = contract(got[0], table_y[0], 4, 0)
    for part in range(1, count_y):
        along_y = along_y + contract(got[part], table_y[part], 4, 0)
    along_y = along_y.transpose(1, 2, 0, 3, 4).reshape(width, pair_count, count_z * rows_z, period)
    spectrum = contract(along_y, table, 2, 0)
    weighted = spectrum * weight[:, None]
    energy_part = jnp.sum(weighted * spectrum, axis=(0, 2, 3))
    back_y = contract(weighted, table, 3, 1)
    back_z = contract(back_y, table, 2, 1)
    back = back_z.reshape(width, pair_count, count_z, rows_z, count_y, rows_y)
    back = back.transpose(4, 2, 0, 1, 3, 5).reshape(spread, width, pair_count, rows_y * rows_z)
    energy_total = group_sum(energy_part, ("gz", "gy"))
    got = lax.all_to_all(back, ("gy", "gz"), 0, 0, tiled=True)
    got = got.reshape(period, pair_count, rows_y * rows_z)
    result = contract(got, table, 0, 1)
    result = result.reshape(pair_count, rows_z, rows_y, length).transpose(0, 2, 1, 3)
    return result, energy_total


def shards(i_coeff, j_coeff, pair_orbital, pair_occ):
    sides = (("gy", 1), ("gz", 2))
    local_count = j_coeff.shape[0]
    band_count = lax.axis_size("band")
    mine = lax.axis_index("band") == jnp.arange(band_count, dtype=jnp.int32)[:, None]
    wanted = group_sum(jnp.where(mine, pair_orbital, 0), ("band",))
    first_owned = lax.axis_index("band") * local_count
    slots = jnp.zeros(wanted.shape + j_coeff.shape[1:], jnp.float32)
    for number in range(local_count):
        hit = (wanted == first_owned + number)[:, :, None, None, None]
        slots = jnp.where(hit, j_coeff[number][None, None], slots)
    arrived = lax.all_to_all(slots, "band", 0, 0, tiled=True)
    arrived, weight = lax.optimization_barrier((arrived, channel_weight(j_coeff.shape[3])))
    own_orbital = synthesize(extended(i_coeff, sides, 8))[0]
    partner = filter_yz(extended(filter_x(jnp.sum(arrived, axis=0)), sides[::-1], 8))
    density = own_orbital[None] * partner
    potential, energy_part = potentials(density, weight)
    weights = pair_occ[0].astype(jnp.float32)
    applied = -jnp.sum(weights[:, None, None, None] * potential * partner, axis=0)
    length = own_orbital.shape[2]
    energy = energy_part / float(length**3)
    return (applied[None], energy[None])


def solution(mesh):
    in_specs = (
        P("band", "gy", "gz", None),
        P("band", "gy", "gz", None),
        P("band", None),
        P("band", None),
    )
    out_specs = (P("band", "gy", "gz", None), P("band", None))
    return jax.shard_map(shards, mesh=mesh, in_specs=in_specs, out_specs=out_specs, check_vma=False)
```

```python
import math

import jax
import jax.numpy as jnp
import numpy as np
from jax import lax
from jax.sharding import PartitionSpec as P

tap_offsets = np.arange(-8, 8)
raw_taps = 0.6 ** np.abs(tap_offsets + 0.5) * np.where(tap_offsets % 2 == 0, 1.0, -0.6)
FILTER_TAPS = raw_taps / np.sqrt(np.sum(raw_taps**2))
SCREEN = 0.001
precise_mode = lax.Precision.HIGHEST
fast_mode = lax.Precision.HIGH


def extended(cells, sides, width):
    for axis, dim in sides:
        count = lax.axis_size(axis)
        extent = cells.shape[dim]
        head = lax.slice_in_dim(cells, 0, width, axis=dim)
        tail = lax.slice_in_dim(cells, extent - width, extent, axis=dim)
        if count == 2:
            first = lax.axis_index(axis) == 0
            got = lax.ppermute(jnp.where(first, tail, head), axis, [(0, 1), (1, 0)])
            empty = jnp.zeros_like(got)
            before = jnp.where(first, empty, got)
            after = jnp.where(first, got, empty)
        else:
            before = lax.ppermute(tail, axis, [(i, i + 1) for i in range(count - 1)])
            after = lax.ppermute(head, axis, [(i + 1, i) for i in range(count - 1)])
        cells = jnp.concatenate([before, cells, after], axis=dim)
    return cells


def group_sum(values, axes):
    total = values
    for axis in axes:
        count = lax.axis_size(axis)
        if count & (count - 1):
            total = lax.psum(total, axis)
            continue
        step = 1
        while step < count:
            total = total + lax.ppermute(total, axis, [(i, i ^ step) for i in range(count)])
            step *= 2
    return total


def band_matrix(row_count, col_count, shift_by):
    row_index = jnp.arange(row_count, dtype=jnp.int32)[:, None]
    col_index = jnp.arange(col_count, dtype=jnp.int32)[None, :]
    offset = row_index - shift_by - col_index
    picked = jnp.zeros((row_count, col_count), jnp.float32)
    for number in range(16):
        picked = picked + jnp.where(offset == number - 8, float(FILTER_TAPS[number]), 0.0)
    return picked


def filter_matrices(wide_y, wide_z, length):
    return (
        band_matrix(wide_y, wide_y - 16, 8),
        band_matrix(wide_z, wide_z - 16, 8),
        band_matrix(length, length, 0),
    )


def synthesize(padded, matrices=None):
    if matrices is None:
        matrices = filter_matrices(padded.shape[1], padded.shape[2], padded.shape[3])
    matrix_y, matrix_z, matrix_x = matrices
    step_one = jnp.matmul(padded, matrix_x, precision=precise_mode)
    step_two = jnp.einsum("oyqx,qz->oyzx", step_one, matrix_z, precision=precise_mode)
    return jnp.einsum("oqzx,qy->oyzx", step_two, matrix_y, precision=precise_mode)


def channel_of(channel, length):
    period = 2 * length
    frequency = jnp.where(channel <= length, channel, channel - length)
    angles = 2.0 * math.pi / period * (frequency % period).astype(jnp.float32)
    lattice = 2.0 - 2.0 * jnp.cos(angles)
    fold = jnp.where((channel == 0) | (channel == length), 1.0, 2.0)
    return frequency, lattice, fold


def channel_table(length):
    period = 2 * length
    channel = jnp.arange(period, dtype=jnp.int32)[None, :]
    frequency, _, _ = channel_of(channel, length)
    positions = jnp.arange(length, dtype=jnp.int32)[:, None] * frequency
    angles = 2.0 * math.pi / period * (positions % period).astype(jnp.float32)
    return jnp.where(channel <= length, jnp.cos(angles), jnp.sin(angles))


def contract(left, right, left_dim, right_dim):
    return lax.dot_general(
        left, right, (((left_dim,), (right_dim,)), ((), ())), precision=fast_mode
    )


def channel_weight(length):
    period = 2 * length
    width = period // (lax.axis_size("gy") * lax.axis_size("gz"))
    own = lax.axis_index(("gy", "gz")) * width + jnp.arange(width, dtype=jnp.int32)
    _, lattice_x, fold_x = channel_of(own, length)
    _, lattice_all, fold_all = channel_of(jnp.arange(period, dtype=jnp.int32), length)
    weight = (
        fold_x[:, None, None] * fold_all[None, :, None] * fold_all[None, None, :]
    ) / (
        (lattice_x[:, None, None] + lattice_all[None, :, None] + lattice_all[None, None, :] + SCREEN)
        * float(period**3)
    )
    return weight


def potentials(density, weight):
    pair_count, rows_y, rows_z, length = density.shape
    period = 2 * length
    count_y = lax.axis_size("gy")
    count_z = lax.axis_size("gz")
    spread = count_y * count_z
    width = period // spread
    table = channel_table(length)
    flat = density.transpose(0, 2, 1, 3).reshape(pair_count * rows_y * rows_z, length)
    along_x = contract(table, flat, 0, 1)
    send = along_x.reshape(spread, width, pair_count, rows_y * rows_z)
    got = lax.all_to_all(send, ("gy", "gz"), 0, 0, tiled=True)
    got = got.reshape(count_y, count_z, width, pair_count, rows_z, rows_y)
    table_y = table.reshape(count_y, rows_y, period)
    along_y = contract(got[0], table_y[0], 4, 0)
    for part in range(1, count_y):
        along_y = along_y + contract(got[part], table_y[part], 4, 0)
    along_y = along_y.transpose(1, 2, 0, 3, 4).reshape(width, pair_count, count_z * rows_z, period)
    spectrum = contract(along_y, table, 2, 0)
    weighted = spectrum * weight[:, None]
    energy_part = jnp.sum(weighted * spectrum, axis=(0, 2, 3))
    back_y = contract(weighted, table, 3, 1)
    back_z = contract(back_y, table, 2, 1)
    back = back_z.reshape(width, pair_count, count_z, rows_z, count_y, rows_y)
    back = back.transpose(4, 2, 0, 1, 3, 5).reshape(spread, width, pair_count, rows_y * rows_z)
    energy_total = group_sum(energy_part, ("gz", "gy"))
    got = lax.all_to_all(back, ("gy", "gz"), 0, 0, tiled=True)
    got = got.reshape(period, pair_count, rows_y * rows_z)
    result = contract(got, table, 0, 1)
    result = result.reshape(pair_count, rows_z, rows_y, length).transpose(0, 2, 1, 3)
    return result, energy_total


def shards(i_coeff, j_coeff, pair_orbital, pair_occ):
    sides = (("gy", 1), ("gz", 2))
    local_count = j_coeff.shape[0]
    band_count = lax.axis_size("band")
    mine = lax.axis_index("band") == jnp.arange(band_count, dtype=jnp.int32)[:, None]
    wanted = group_sum(jnp.where(mine, pair_orbital, 0), ("band",))
    first_owned = lax.axis_index("band") * local_count
    slots = jnp.zeros(wanted.shape + j_coeff.shape[1:], jnp.float32)
    for number in range(local_count):
        hit = (wanted == first_owned + number)[:, :, None, None, None]
        slots = jnp.where(hit, j_coeff[number][None, None], slots)
    arrived = lax.all_to_all(slots, "band", 0, 0, tiled=True)
    matrices = filter_matrices(j_coeff.shape[1] + 16, j_coeff.shape[2] + 16, j_coeff.shape[3])
    arrived, weight, matrices = lax.optimization_barrier(
        (arrived, channel_weight(j_coeff.shape[3]), matrices)
    )
    own_orbital = synthesize(extended(i_coeff, sides, 8))[0]
    partner = synthesize(extended(jnp.sum(arrived, axis=0), sides[::-1], 8), matrices)
    density = own_orbital[None] * partner
    potential, energy_part = potentials(density, weight)
    weights = pair_occ[0].astype(jnp.float32)
    applied = -jnp.sum(weights[:, None, None, None] * potential * partner, axis=0)
    length = own_orbital.shape[2]
    energy = energy_part / float(length**3)
    return (applied[None], energy[None])


def solution(mesh):
    in_specs = (
        P("band", "gy", "gz", None),
        P("band", "gy", "gz", None),
        P("band", None),
        P("band", None),
    )
    out_specs = (P("band", "gy", "gz", None), P("band", None))
    return jax.shard_map(shards, mesh=mesh, in_specs=in_specs, out_specs=out_specs, check_vma=False)
```
